512 devices in a mesh: req: 128 (over y, z, core), tp: 4 (over x).
Axes of the slice: x: 4, y: 8, z: 8, core: 2. Of those that a mesh axis runs over, the one named last changes fastest.
Arguments:
- qkv_rows: bfloat16 [32768, 3, 1536], P('req', None, 'tp'), may hold values from -13 to 13
- row_request: int32 [32768], P('req'), may hold values from 0 to 127, as said below
- request_owner: int32 [128], replicated, may hold values from 0 to 127, each once
- cached_len: int32 [128], P('req'), may hold values from 0 to 1024
- page_table: int32 [128, 8], P('req'), may hold values from 0 to 7, as said below
- kv_pages: bfloat16 [1024, 2, 128, 1536], P('req', None, None, 'tp'), may hold values from -6 to 6
- residual: bfloat16 [32768, 3072], P('req', 'tp'), may hold values from -128 to 128
- out_weight: bfloat16 [1536, 3072], P('tp'), may hold values from -0.15625 to 0.15625
- norm_gain: bfloat16 [3072], P('tp'), may hold values from 0.5 to 1.5
Outputs:
- new_residual: bfloat16 [32768, 3072], P('req', 'tp')
- normed: bfloat16 [32768, 3072], P('req', 'tp')
The draws below stay inside these ranges and needn't reach their ends.
Inputs may be any that keep to these rules, and one draw needn't show every extreme that they name: `row_request`: on every device at most 5 new tokens name the same request, and one request is named by exactly 5 tokens on every device. Half of the requests are named by exactly one token in all, and no two of those tokens lie on one device. `request_owner`: each device holds the cache of exactly one request. `page_table`: each row names every page of its device's pool once.
All inputs are finite; a program needn't handle non-finite values.
Results may differ from the reference program's by a relative error of at most 0.0093.
The reference program's roundings to bfloat16 on the way count: a program that leaves them out, or rounds other values in their place, can miss the bound.
Values may be sent and summed in bfloat16 or wider, within the bound.
No kernel may reach another device: no remote copies, remote signals or barrier semaphores. Data moves between devices by JAX's collectives and lax.ppermute only.
A program may use at most 64 MiB of HBM per device.

```python
import math
import jax
import jax.numpy as jnp
from jax import lax

D = 3072
HEAD_SIZE = 96
HEADS = 16
PAGE = 128
MAXP = 8
TOK_DEV = 256
HC = 1536
SLOT = 5
TOKENS = 32768
N_REQ = 128


def draw_row_request(key, part):
    half_reqs = N_REQ // 2
    entries = half_reqs * SLOT
    key_order, key_block, key_caps, key_rows = jax.random.split(key, 4)
    request_order = jax.random.permutation(key_order, N_REQ).astype(jnp.int32)
    decoders = request_order[:half_reqs]
    prefills = request_order[half_reqs:]
    decode_block = jax.random.permutation(key_block, N_REQ).astype(jnp.int32)[:half_reqs]
    lowest = (SLOT + 1) // 2
    capacity = jax.random.randint(key_caps, (half_reqs,), lowest, SLOT + 1).astype(jnp.int32).at[0].set(SLOT)
    entry_request = jnp.repeat(prefills, SLOT)
    entry_copy = jnp.tile(jnp.arange(SLOT, dtype=jnp.int32), half_reqs)
    entry_valid = entry_copy < jnp.repeat(capacity, SLOT)
    entry_first = jnp.repeat(jnp.arange(half_reqs) == 0, SLOT)
    decode_index = jnp.arange(half_reqs, dtype=jnp.int32)

    def one_block(number):
        key_here = jax.random.fold_in(key_rows, number)
        key_noise, key_shuffle = jax.random.split(key_here)
        noise_rank = jax.random.permutation(key_noise, entries).astype(jnp.int32)
        prefill_score = jnp.where(entry_first, entry_copy - SLOT, jnp.where(entry_valid, noise_rank, entries + noise_rank))
        decode_score = jnp.where(decode_block == number, decode_index - half_reqs - SLOT, 2 * entries + decode_index)
        logit_scores = jnp.concatenate([decode_score, prefill_score])
        candidates = jnp.concatenate([decoders, entry_request])
        chosen = candidates[jnp.argsort(logit_scores)][:TOK_DEV]
        return chosen[jax.random.permutation(key_shuffle, TOK_DEV)]
    return jax.vmap(one_block)(jnp.arange(N_REQ, dtype=jnp.int32)).reshape(N_REQ * TOK_DEV).astype(jnp.int32)


def draw_cached_len(key, part):
    key_len, key_full = jax.random.split(key)
    most_len = MAXP * PAGE
    lengths = jax.random.randint(key_len, (N_REQ,), 0, most_len + 1).astype(jnp.int32)
    longest = jax.random.randint(key_full, (), 0, N_REQ)
    return lengths.at[longest].set(most_len).astype(jnp.int32)


def draw_page_table(key, part):

    def one_row(number):
        return jax.random.permutation(jax.random.fold_in(key, number), MAXP)
    return jax.vmap(one_row)(jnp.arange(N_REQ, dtype=jnp.int32)).astype(jnp.int32)


def draw_qkv_rows(key, part):
    key_base = jax.random.fold_in(key, 0)
    shape_all = (TOKENS, 3, HEADS * HEAD_SIZE)
    return jnp.clip(jax.random.normal(key_base, shape_all, jnp.float32), -6.0, 6.0).astype(jnp.bfloat16)


def draw_residual(key, part):
    key_base, key_row, key_col = jax.random.split(key, 3)
    column = jnp.arange(D, dtype=jnp.float32) / (D - 1)
    base_vals = jnp.clip(jax.random.normal(key_base, (TOKENS, D), jnp.float32), -4.0, 4.0)
    row_scale = jnp.exp(jax.random.uniform(key_row, (TOKENS, 1), jnp.float32, jnp.log(0.2), jnp.log(2.0)))
    ramp_cols = (1.0 + 2.0 * column) / 2.0
    col_scale = jnp.exp(jax.random.uniform(key_col, (1, D), jnp.float32, jnp.log(0.3), jnp.log(3.0)))
    return (base_vals * row_scale * col_scale * ramp_cols[None, :]).astype(jnp.bfloat16)


def block_scale(key, extent, cuts, low, largest):
    def one(dim, blocks):
        steps = jax.random.uniform(jax.random.fold_in(jax.random.fold_in(key, 6), dim), (blocks,), jnp.float32, low / len(cuts), largest / len(cuts))
        return jnp.repeat(jnp.exp(steps), extent[dim] // blocks).reshape((-1,) + (1,) * (len(extent) - dim - 1))

    gain = one(*cuts[0])
    for cut in cuts[1:]:
        gain = gain * one(*cut)
    return gain


def bell_draw(own_key, extent, width, reach, cuts=(), kind=jnp.bfloat16):
    factor_of = block_scale(own_key, extent, cuts, -0.22, 0.18) if cuts else 1.0
    values = jax.random.normal(own_key, extent, jnp.float32) * width * factor_of
    return jnp.minimum(jnp.maximum(values, -reach), reach).astype(kind)


def setup_inputs(seed: int = 0) -> dict:
    key_list = jax.random.split(jax.random.key(seed), 10)
    return {
        "qkv_rows": draw_qkv_rows(jax.random.fold_in(key_list[9], 71), 0),
        "row_request": draw_row_request(jax.random.fold_in(key_list[9], 71), 0),
        "request_owner": jax.random.permutation(key_list[2], N_REQ).astype(jnp.int32),
        "cached_len": draw_cached_len(jax.random.fold_in(key_list[9], 71), 0),
        "page_table": draw_page_table(jax.random.fold_in(key_list[9], 71), 0),
        "kv_pages": bell_draw(key_list[5], (N_REQ * MAXP, 2, PAGE, HC), 1.0, 6.0, ((0, 128), (3, 4))),
        "residual": draw_residual(jax.random.fold_in(key_list[9], 71), 0),
        "out_weight": bell_draw(key_list[7], (HC, D), HC ** -0.5, 0.15625, ((0, 4),)),
        "norm_gain": jnp.clip(1.0 + 0.1 * jax.random.normal(key_list[8], (D,), jnp.float32), 0.5, 1.5).astype(jnp.bfloat16),
    }


ROPE_BASE = 10000.0
EPS = 1e-05

def rope_tables(position):
    halves = HEAD_SIZE // 2
    inverse = ROPE_BASE ** (-2.0 * jnp.arange(halves, dtype=jnp.float32) / HEAD_SIZE)
    angles = position.astype(jnp.float32)[:, None] * inverse[None, :]
    cosine = jnp.concatenate([jnp.cos(angles), jnp.cos(angles)], axis=1)
    sine_tab = jnp.concatenate([jnp.sin(angles), jnp.sin(angles)], axis=1)
    return (cosine, sine_tab)

def rotate(field, cosine, sine_tab):
    halves = HEAD_SIZE // 2
    turned = jnp.concatenate([-field[..., halves:], field[..., :halves]], axis=-1)
    return field * cosine[:, None, :] + turned * sine_tab[:, None, :]

def attend(query_rows_block, gathered_keys, gathered_values, visible):
    logit_scores = jnp.einsum('bso,aso->sba', query_rows_block.astype(jnp.float32), gathered_keys.astype(jnp.float32)) * (1.0 / math.sqrt(HEAD_SIZE))
    logit_scores = jnp.where(visible[None, :, :], logit_scores, -1e+30)
    top_score = lax.optimization_barrier(jnp.max(logit_scores, axis=2, keepdims=True))
    weight = jnp.exp(logit_scores - top_score)
    softmax_weights = (weight / lax.optimization_barrier(jnp.sum(weight, axis=2, keepdims=True))).astype(jnp.bfloat16)
    attended_output = jnp.einsum('pyg,gpc->ypc', softmax_weights.astype(jnp.float32), gathered_values.astype(jnp.float32))
    return attended_output.astype(jnp.bfloat16)

def reference(qkv_rows, row_request, request_owner, cached_len, page_table, kv_pages, residual, out_weight, norm_gain):
    total_rows = qkv_rows.shape[0]
    requests = request_owner.shape[0]
    most_rows = SLOT * N_REQ
    cache_span = MAXP * PAGE
    matches = (row_request[:, None] == jnp.arange(requests, dtype=jnp.int32)[None, :]).astype(jnp.int32)
    earlier = (jnp.cumsum(matches, axis=0) - matches).astype(jnp.int32)
    rank_all = lax.optimization_barrier(jnp.sum(earlier * matches, axis=1)).astype(jnp.int32)
    counts = lax.optimization_barrier(jnp.sum(matches, axis=0)).astype(jnp.int32)
    row_table = jnp.full((requests, most_rows), total_rows, jnp.int32)
    row_table = row_table.at[row_request, rank_all].set(jnp.arange(total_rows, dtype=jnp.int32))

    def one_request(number):
        row_ids = row_table[number]
        slot_ids = jnp.arange(most_rows, dtype=jnp.int32)
        live_slot = slot_ids < counts[number]
        safe_rows = jnp.minimum(row_ids, total_rows - 1)
        grouped = qkv_rows[safe_rows].reshape(most_rows, 3, HEADS, HEAD_SIZE)
        holder = request_owner[number].astype(jnp.int32)
        length = cached_len[holder].astype(jnp.int32)
        position = (length + slot_ids).astype(jnp.int32)
        cosine, sine_tab = rope_tables(position)
        query_rows_block = rotate(grouped[:, 0].astype(jnp.float32), cosine, sine_tab).astype(jnp.bfloat16)
        fresh_keys = rotate(grouped[:, 1].astype(jnp.float32), cosine, sine_tab).astype(jnp.bfloat16)
        pool_pages = lax.dynamic_slice_in_dim(kv_pages, (holder * MAXP).astype(jnp.int32), MAXP, 0)
        pool_pages = pool_pages[page_table[holder]]
        cache_keys = pool_pages[:, 0].reshape(cache_span, HEADS, HEAD_SIZE)
        cache_values = pool_pages[:, 1].reshape(cache_span, HEADS, HEAD_SIZE)
        gathered_keys = jnp.concatenate([cache_keys, fresh_keys], axis=0)
        gathered_values = jnp.concatenate([cache_values, grouped[:, 2]], axis=0)
        cache_ok = jnp.broadcast_to((jnp.arange(cache_span, dtype=jnp.int32) < length)[None, :], (most_rows, cache_span))
        new_ok = live_slot[None, :] & (slot_ids[None, :] <= slot_ids[:, None])
        visible = jnp.concatenate([cache_ok, new_ok], axis=1)
        return attend(query_rows_block, gathered_keys, gathered_values, visible).reshape(most_rows, HC)
    outputs = lax.map(one_request, jnp.arange(requests, dtype=jnp.int32))
    attn_rows = jnp.zeros((total_rows + 1, HC), jnp.bfloat16).at[row_table.reshape(-1)].set(outputs.reshape(-1, HC))[:total_rows]
    mixed_cols = jnp.dot(attn_rows, out_weight, preferred_element_type=jnp.float32)
    hidden = residual.astype(jnp.float32) + mixed_cols
    square_mean = lax.optimization_barrier(jnp.mean(hidden * hidden, axis=1, keepdims=True))
    normed = hidden * lax.rsqrt(square_mean + EPS) * norm_gain.astype(jnp.float32)[None, :]
    return (hidden.astype(jnp.bfloat16), normed.astype(jnp.bfloat16))
```

```python
import math

import jax
import jax.numpy as jnp
from jax import lax
from jax.sharding import PartitionSpec as P

D = 3072
HEAD_SIZE = 96
SLOT = 5

ROPE_BASE = 10000.0
EPS = 1e-05


def rope_tables(position):
    halves = HEAD_SIZE // 2
    inverse = ROPE_BASE ** (-2.0 * jnp.arange(halves, dtype=jnp.float32) / HEAD_SIZE)
    angles = position.astype(jnp.float32)[:, None] * inverse[None, :]
    cosine = jnp.concatenate([jnp.cos(angles), jnp.cos(angles)], axis=1)
    sine_tab = jnp.concatenate([jnp.sin(angles), jnp.sin(angles)], axis=1)
    return (cosine, sine_tab)


def rotate(field, cosine, sine_tab):
    halves = HEAD_SIZE // 2
    turned = jnp.concatenate([-field[..., halves:], field[..., :halves]], axis=-1)
    return field * cosine[:, None, :] + turned * sine_tab[:, None, :]


def attend_heads(grouped, cache_keys, cache_values, cosine, sine_tab, visible):
    score_scale = 1.0 / math.sqrt(HEAD_SIZE)
    query_rows_block = rotate(grouped[:, 0].astype(jnp.float32), cosine, sine_tab).astype(
        jnp.bfloat16
    )
    fresh_keys = rotate(grouped[:, 1].astype(jnp.float32), cosine, sine_tab).astype(jnp.bfloat16)
    gathered_keys = jnp.concatenate([cache_keys, fresh_keys], axis=0)
    gathered_values = jnp.concatenate([cache_values, grouped[:, 2]], axis=0)

    def one_head(head_parts):
        head_query, head_keys, head_values = head_parts
        logit_scores = (
            jnp.einsum("md,kd->mk", head_query, head_keys, preferred_element_type=jnp.float32)
            * score_scale
        )
        logit_scores = jnp.where(visible, logit_scores, -1e30)
        top_score = jnp.max(logit_scores, axis=1, keepdims=True)
        weight = jnp.exp(logit_scores - top_score)
        softmax_weights = (weight / jnp.sum(weight, axis=1, keepdims=True)).astype(jnp.bfloat16)
        return jnp.einsum(
            "mk,kd->md", softmax_weights, head_values, preferred_element_type=jnp.float32
        ).astype(jnp.bfloat16)

    heads_out = lax.map(
        one_head,
        (
            query_rows_block.transpose(1, 0, 2),
            gathered_keys.transpose(1, 0, 2),
            gathered_values.transpose(1, 0, 2),
        ),
    )
    return heads_out.transpose(1, 0, 2)


def on_device(
    qkv_rows,
    row_request,
    request_owner,
    cached_len,
    page_table,
    kv_pages,
    residual,
    out_weight,
    norm_gain,
):
    row_count = qkv_rows.shape[0]
    parts = qkv_rows.shape[1]
    head_cols = qkv_rows.shape[2]
    heads_here = head_cols // HEAD_SIZE
    devices = lax.axis_size("req")
    slot_cap = SLOT
    buffer_len = devices * slot_cap
    device_ids = jnp.arange(devices, dtype=jnp.int32)
    row_ids = jnp.arange(row_count, dtype=jnp.int32)

    owner_dev = request_owner[row_request]
    same_owner = owner_dev[:, None] == owner_dev[None, :]
    slot_in = jnp.sum((same_owner & (row_ids[None, :] < row_ids[:, None])).astype(jnp.int32), axis=1)
    sends_to = owner_dev[:, None] == device_ids[None, :]
    counts = jnp.sum(sends_to.astype(jnp.int32), axis=0)

    pick = (
        sends_to[None, :, :]
        & (slot_in[None, :, None] == jnp.arange(slot_cap, dtype=jnp.int32)[:, None, None])
    ).astype(jnp.bfloat16)
    slots = jnp.einsum(
        "jid,ipc->djpc", pick, qkv_rows, preferred_element_type=jnp.float32
    ).astype(jnp.bfloat16)
    count_row = jnp.broadcast_to(counts.astype(jnp.bfloat16)[:, None, None], (devices, 1, head_cols))
    outgoing = jnp.concatenate(
        [slots.reshape(devices, slot_cap * parts, head_cols), count_row], axis=1
    )
    arrived = lax.all_to_all(outgoing, "req", split_axis=0, concat_axis=0, tiled=True)
    arrived_counts = arrived[:, slot_cap * parts, 0].astype(jnp.int32)

    length = cached_len[0]
    pool_pages = kv_pages[page_table[0]]
    cache_span = pool_pages.shape[0] * pool_pages.shape[2]
    cache_keys = pool_pages[:, 0].reshape(cache_span, heads_here, HEAD_SIZE)
    cache_values = pool_pages[:, 1].reshape(cache_span, heads_here, HEAD_SIZE)
    live_slot = (jnp.arange(slot_cap, dtype=jnp.int32)[None, :] < arrived_counts[:, None]).reshape(
        buffer_len
    )
    live_int = live_slot.astype(jnp.int32)
    new_rank = jnp.cumsum(live_int) - live_int
    cosine, sine_tab = rope_tables(length + new_rank)
    cache_ok = jnp.broadcast_to(
        (jnp.arange(cache_span, dtype=jnp.int32) < length)[None, :], (buffer_len, cache_span)
    )
    new_ok = live_slot[None, :] & (new_rank[None, :] <= new_rank[:, None])
    visible = jnp.concatenate([cache_ok, new_ok], axis=1)
    grouped = arrived[:, : slot_cap * parts].reshape(buffer_len, parts, heads_here, HEAD_SIZE)
    result = attend_heads(grouped, cache_keys, cache_values, cosine, sine_tab, visible)
    returned = lax.all_to_all(
        result.reshape(devices, slot_cap * head_cols), "req", split_axis=0, concat_axis=0, tiled=True
    )
    target = owner_dev * slot_cap + slot_in
    attn_rows = returned.reshape(buffer_len, head_cols)[target]
    partial_sum = jnp.dot(attn_rows, out_weight, preferred_element_type=jnp.float32)
    mixed_cols = lax.psum_scatter(
        partial_sum.astype(jnp.bfloat16), "tp", scatter_dimension=1, tiled=True
    ).astype(jnp.float32)
    hidden = residual.astype(jnp.float32) + mixed_cols
    square_sum = lax.psum(jnp.sum(hidden * hidden, axis=1), "tp")
    inv_rms = lax.rsqrt(square_sum / D + EPS)
    normed = hidden * inv_rms[:, None] * norm_gain.astype(jnp.float32)[None, :]
    return (hidden.astype(jnp.bfloat16), normed.astype(jnp.bfloat16))


def solution(mesh):
    return jax.shard_map(
        on_device,
        mesh=mesh,
        in_specs=(
            P("req", None, "tp"),
            P("req"),
            P(),
            P("req"),
            P("req", None),
            P("req", None, None, "tp"),
            P("req", "tp"),
            P("tp", None),
            P("tp"),
        ),
        out_specs=(P("req", "tp"), P("req", "tp")),
        check_vma=False,
    )
```

```python
import math

import jax
import jax.numpy as jnp
from jax import lax
from jax.sharding import PartitionSpec as P

D = 3072
HEAD_SIZE = 96
SLOT = 5
REQ = ("ry", "rz", "rc")
OUTER = 8

ROPE_BASE = 10000.0
EPS = 1e-05


def rope_tables(position):
    halves = HEAD_SIZE // 2
    inverse = ROPE_BASE ** (-2.0 * jnp.arange(halves, dtype=jnp.float32) / HEAD_SIZE)
    angles = position.astype(jnp.float32)[:, None] * inverse[None, :]
    cosine = jnp.concatenate([jnp.cos(angles), jnp.cos(angles)], axis=1)
    sine_tab = jnp.concatenate([jnp.sin(angles), jnp.sin(angles)], axis=1)
    return (cosine, sine_tab)


def rotate(field, cosine, sine_tab):
    halves = HEAD_SIZE // 2
    turned = jnp.concatenate([-field[..., halves:], field[..., :halves]], axis=-1)
    return field * cosine[:, None, :] + turned * sine_tab[:, None, :]


def attend_heads(grouped, cache_keys, cache_values, cosine, sine_tab, visible):
    score_scale = 1.0 / math.sqrt(HEAD_SIZE)
    query_rows_block = rotate(grouped[:, 0].astype(jnp.float32), cosine, sine_tab).astype(
        jnp.bfloat16
    )
    fresh_keys = rotate(grouped[:, 1].astype(jnp.float32), cosine, sine_tab).astype(jnp.bfloat16)
    gathered_keys = jnp.concatenate([cache_keys, fresh_keys], axis=0)
    gathered_values = jnp.concatenate([cache_values, grouped[:, 2]], axis=0)

    def one_head(head_parts):
        head_query, head_keys, head_values = head_parts
        logit_scores = (
            jnp.einsum("md,kd->mk", head_query, head_keys, preferred_element_type=jnp.float32)
            * score_scale
        )
        logit_scores = jnp.where(visible, logit_scores, -1e30)
        top_score = jnp.max(logit_scores, axis=1, keepdims=True)
        weight = jnp.exp(logit_scores - top_score)
        softmax_weights = (weight / jnp.sum(weight, axis=1, keepdims=True)).astype(jnp.bfloat16)
        return jnp.einsum(
            "mk,kd->md", softmax_weights, head_values, preferred_element_type=jnp.float32
        ).astype(jnp.bfloat16)

    heads_out = lax.map(
        one_head,
        (
            query_rows_block.transpose(1, 0, 2),
            gathered_keys.transpose(1, 0, 2),
            gathered_values.transpose(1, 0, 2),
        ),
    )
    return heads_out.transpose(1, 0, 2)


def two_stage_all_to_all(x):
    devices = x.shape[0]
    inner = devices // OUTER
    x = x.reshape((OUTER, inner) + x.shape[1:])
    x = lax.all_to_all(x, "ry", split_axis=0, concat_axis=0, tiled=True)
    x = lax.all_to_all(x, ("rz", "rc"), split_axis=1, concat_axis=1, tiled=True)
    return x.reshape((devices,) + x.shape[2:])


def on_device(
    qkv_rows,
    row_request,
    request_owner,
    cached_len,
    page_table,
    kv_pages,
    residual,
    out_weight,
    norm_gain,
):
    row_count = qkv_rows.shape[0]
    parts = qkv_rows.shape[1]
    head_cols = qkv_rows.shape[2]
    heads_here = head_cols // HEAD_SIZE
    devices = lax.axis_size(REQ)
    slot_cap = SLOT
    buffer_len = devices * slot_cap
    device_ids = jnp.arange(devices, dtype=jnp.int32)
    row_ids = jnp.arange(row_count, dtype=jnp.int32)

    owner_dev = request_owner[row_request]
    same_owner = owner_dev[:, None] == owner_dev[None, :]
    slot_in = jnp.sum((same_owner & (row_ids[None, :] < row_ids[:, None])).astype(jnp.int32), axis=1)
    sends_to = owner_dev[:, None] == device_ids[None, :]
    counts = jnp.sum(sends_to.astype(jnp.int32), axis=0)

    pick = (
        sends_to[None, :, :]
        & (slot_in[None, :, None] == jnp.arange(slot_cap, dtype=jnp.int32)[:, None, None])
    ).astype(jnp.bfloat16)
    slots = jnp.einsum(
        "jid,ipc->djpc", pick, qkv_rows, preferred_element_type=jnp.float32
    ).astype(jnp.bfloat16)
    count_row = jnp.broadcast_to(counts.astype(jnp.bfloat16)[:, None, None], (devices, 1, head_cols))
    outgoing = jnp.concatenate(
        [slots.reshape(devices, slot_cap * parts, head_cols), count_row], axis=1
    )
    arrived = two_stage_all_to_all(outgoing)
    arrived_counts = arrived[:, slot_cap * parts, 0].astype(jnp.int32)

    length = cached_len[0]
    pool_pages = kv_pages[page_table[0]]
    cache_span = pool_pages.shape[0] * pool_pages.shape[2]
    cache_keys = pool_pages[:, 0].reshape(cache_span, heads_here, HEAD_SIZE)
    cache_values = pool_pages[:, 1].reshape(cache_span, heads_here, HEAD_SIZE)
    live_slot = (jnp.arange(slot_cap, dtype=jnp.int32)[None, :] < arrived_counts[:, None]).reshape(
        buffer_len
    )
    live_int = live_slot.astype(jnp.int32)
    new_rank = jnp.cumsum(live_int) - live_int
    cosine, sine_tab = rope_tables(length + new_rank)
    cache_ok = jnp.broadcast_to(
        (jnp.arange(cache_span, dtype=jnp.int32) < length)[None, :], (buffer_len, cache_span)
    )
    new_ok = live_slot[None, :] & (new_rank[None, :] <= new_rank[:, None])
    visible = jnp.concatenate([cache_ok, new_ok], axis=1)
    grouped = arrived[:, : slot_cap * parts].reshape(buffer_len, parts, heads_here, HEAD_SIZE)
    result = attend_heads(grouped, cache_keys, cache_values, cosine, sine_tab, visible)
    returned = two_stage_all_to_all(result.reshape(devices, slot_cap * parts, head_cols // parts))
    target = owner_dev * slot_cap + slot_in
    attn_rows = returned.reshape(buffer_len, head_cols)[target]
    partial_sum = jnp.dot(attn_rows, out_weight, preferred_element_type=jnp.float32)
    mixed_cols = lax.psum_scatter(
        partial_sum.astype(jnp.bfloat16), "tp", scatter_dimension=1, tiled=True
    ).astype(jnp.float32)
    hidden = residual.astype(jnp.float32) + mixed_cols
    square_sum = lax.psum(jnp.sum(hidden * hidden, axis=1), "tp")
    inv_rms = lax.rsqrt(square_sum / D + EPS)
    normed = hidden * inv_rms[:, None] * norm_gain.astype(jnp.float32)[None, :]
    return (hidden.astype(jnp.bfloat16), normed.astype(jnp.bfloat16))


def solution(mesh):
    req_size = mesh.shape["req"]
    split_mesh = jax.sharding.Mesh(
        mesh.devices.reshape(OUTER, req_size // OUTER // 2, 2, mesh.shape["tp"]),
        REQ + ("tp",),
    )
    return jax.shard_map(
        on_device,
        mesh=split_mesh,
        in_specs=(
            P(REQ, None, "tp"),
            P(REQ),
            P(),
            P(REQ),
            P(REQ, None),
            P(REQ, None, None, "tp"),
            P(REQ, "tp"),
            P("tp", None),
            P("tp"),
        ),
        out_specs=(P(REQ, "tp"), P(REQ, "tp")),
        check_vma=False,
    )
```

```python
import math

import jax
import jax.numpy as jnp
from jax import lax
from jax.sharding import PartitionSpec as P

D = 3072
HEAD_SIZE = 96
SLOT = 5

ROPE_BASE = 10000.0
EPS = 1e-05


def rope_tables(position):
    halves = HEAD_SIZE // 2
    inverse = ROPE_BASE ** (-2.0 * jnp.arange(halves, dtype=jnp.float32) / HEAD_SIZE)
    angles = position.astype(jnp.float32)[:, None] * inverse[None, :]
    cosine = jnp.concatenate([jnp.cos(angles), jnp.cos(angles)], axis=1)
    sine_tab = jnp.concatenate([jnp.sin(angles), jnp.sin(angles)], axis=1)
    return (cosine, sine_tab)


def rotate(field, cosine, sine_tab):
    halves = HEAD_SIZE // 2
    turned = jnp.concatenate([-field[..., halves:], field[..., :halves]], axis=-1)
    return field * cosine[:, None, :] + turned * sine_tab[:, None, :]


def turn_matrix(cols):
    halves = HEAD_SIZE // 2
    c_in = jnp.arange(cols, dtype=jnp.int32)[:, None]
    c_out = jnp.arange(cols, dtype=jnp.int32)[None, :]
    local = c_out % HEAD_SIZE
    same_head = (c_in // HEAD_SIZE) == (c_out // HEAD_SIZE)
    low = same_head & (local < halves) & (c_in % HEAD_SIZE == local + halves)
    high = same_head & (local >= halves) & (c_in % HEAD_SIZE == local - halves)
    return jnp.where(low, -1.0, jnp.where(high, 1.0, 0.0)).astype(jnp.bfloat16)


def rotate_flat(field, cosine, sine_tab, turn):
    heads = field.shape[1] // HEAD_SIZE
    turned = jnp.dot(field, turn, preferred_element_type=jnp.float32)
    cos_all = jnp.tile(cosine, (1, heads))
    sin_all = jnp.tile(sine_tab, (1, heads))
    return (field.astype(jnp.float32) * cos_all + turned * sin_all).astype(jnp.bfloat16)


def attend_flat(query, keys, values, visible):
    score_scale = 1.0 / math.sqrt(HEAD_SIZE)
    cols = query.shape[1]
    col_head = jnp.arange(cols, dtype=jnp.int32) // HEAD_SIZE

    def one_head(head):
        chosen = (col_head == head)[None, :]
        head_query = jnp.where(chosen, query, jnp.zeros_like(query))
        logit_scores = (
            jnp.einsum("mc,kc->mk", head_query, keys, preferred_element_type=jnp.float32)
            * score_scale
        )
        logit_scores = jnp.where(visible, logit_scores, -1e30)
        top_score = jnp.max(logit_scores, axis=1, keepdims=True)
        weight = jnp.exp(logit_scores - top_score)
        softmax_weights = (weight / jnp.sum(weight, axis=1, keepdims=True)).astype(jnp.bfloat16)
        head_out = jnp.einsum(
            "mk,kc->mc", softmax_weights, values, preferred_element_type=jnp.float32
        ).astype(jnp.bfloat16)
        return jnp.where(chosen, head_out, jnp.zeros_like(head_out))

    outs = lax.map(one_head, jnp.arange(cols // HEAD_SIZE, dtype=jnp.int32))
    return jnp.sum(outs, axis=0, dtype=jnp.float32).astype(jnp.bfloat16)


def on_device(
    qkv_rows,
    row_request,
    request_owner,
    cached_len,
    page_table,
    kv_pages,
    residual,
    out_weight,
    norm_gain,
):
    row_count = qkv_rows.shape[0]
    parts = qkv_rows.shape[1]
    head_cols = qkv_rows.shape[2]
    heads_here = head_cols // HEAD_SIZE
    devices = lax.axis_size("req")
    slot_cap = SLOT
    buffer_len = devices * slot_cap
    device_ids = jnp.arange(devices, dtype=jnp.int32)
    row_ids = jnp.arange(row_count, dtype=jnp.int32)

    owner_dev = request_owner[row_request]
    same_owner = owner_dev[:, None] == owner_dev[None, :]
    slot_in = jnp.sum((same_owner & (row_ids[None, :] < row_ids[:, None])).astype(jnp.int32), axis=1)
    sends_to = owner_dev[:, None] == device_ids[None, :]
    counts = jnp.sum(sends_to.astype(jnp.int32), axis=0)

    pick = (
        sends_to[None, :, :]
        & (slot_in[None, :, None] == jnp.arange(slot_cap, dtype=jnp.int32)[:, None, None])
    ).astype(jnp.bfloat16)
    slots = jnp.einsum(
        "jid,ipc->dpjc", pick, qkv_rows, preferred_element_type=jnp.float32
    ).astype(jnp.bfloat16)
    count_row = jnp.broadcast_to(counts.astype(jnp.bfloat16)[:, None, None], (devices, 1, head_cols))
    outgoing = jnp.concatenate(
        [slots.reshape(devices, slot_cap * parts, head_cols), count_row], axis=1
    )
    arrived = lax.all_to_all(outgoing, "req", split_axis=0, concat_axis=0, tiled=True)
    arrived_counts = arrived[:, slot_cap * parts, 0].astype(jnp.int32)

    length = cached_len[0]
    pool_pages = kv_pages[page_table[0]]
    cache_span = pool_pages.shape[0] * pool_pages.shape[2]
    cache_keys = pool_pages[:, 0].reshape(cache_span, head_cols)
    cache_values = pool_pages[:, 1].reshape(cache_span, head_cols)
    live_slot = (jnp.arange(slot_cap, dtype=jnp.int32)[None, :] < arrived_counts[:, None]).reshape(
        buffer_len
    )
    live_int = live_slot.astype(jnp.int32)
    new_rank = jnp.cumsum(live_int) - live_int
    cosine, sine_tab = rope_tables(length + new_rank)
    cache_ok = jnp.broadcast_to(
        (jnp.arange(cache_span, dtype=jnp.int32) < length)[None, :], (buffer_len, cache_span)
    )
    new_ok = live_slot[None, :] & (new_rank[None, :] <= new_rank[:, None])
    visible = jnp.concatenate([cache_ok, new_ok], axis=1)
    part_rows = [
        arrived[:, p * slot_cap : (p + 1) * slot_cap].reshape(buffer_len, head_cols)
        for p in range(parts)
    ]
    turn = turn_matrix(head_cols)
    query = rotate_flat(part_rows[0], cosine, sine_tab, turn)
    fresh_keys = rotate_flat(part_rows[1], cosine, sine_tab, turn)
    keys = jnp.concatenate([cache_keys, fresh_keys], axis=0)
    values = jnp.concatenate([cache_values, part_rows[2]], axis=0)
    result = attend_flat(query, keys, values, visible)
    returned = lax.all_to_all(
        result.reshape(devices, slot_cap * parts, head_cols // parts),
        "req",
        split_axis=0,
        concat_axis=0,
        tiled=True,
    )
    target = owner_dev * slot_cap + slot_in
    attn_rows = returned.reshape(buffer_len, head_cols)[target]
    partial_sum = jnp.dot(attn_rows, out_weight, preferred_element_type=jnp.float32)
    mixed_cols = lax.psum_scatter(
        partial_sum.astype(jnp.bfloat16), "tp", scatter_dimension=1, tiled=True
    ).astype(jnp.float32)
    hidden = residual.astype(jnp.float32) + mixed_cols
    square_sum = lax.psum(jnp.sum(hidden * hidden, axis=1), "tp")
    inv_rms = lax.rsqrt(square_sum / D + EPS)
    normed = hidden * inv_rms[:, None] * norm_gain.astype(jnp.float32)[None, :]
    return (hidden.astype(jnp.bfloat16), normed.astype(jnp.bfloat16))


def solution(mesh):
    return jax.shard_map(
        on_device,
        mesh=mesh,
        in_specs=(
            P("req", None, "tp"),
            P("req"),
            P(),
            P("req"),
            P("req", None),
            P("req", None, None, "tp"),
            P("req", "tp"),
            P("tp", None),
            P("tp"),
        ),
        out_specs=(P("req", "tp"), P("req", "tp")),
        check_vma=False,
    )
```

```python
import math

import jax
import jax.numpy as jnp
from jax import lax
from jax.experimental import pallas as pl
from jax.experimental.pallas import tpu as pltpu
from jax.sharding import PartitionSpec as P

D = 3072
HEAD_SIZE = 96
SLOT = 5

ROPE_BASE = 10000.0
EPS = 1e-05


def rope_tables(position):
    halves = HEAD_SIZE // 2
    inverse = ROPE_BASE ** (-2.0 * jnp.arange(halves, dtype=jnp.float32) / HEAD_SIZE)
    angles = position.astype(jnp.float32)[:, None] * inverse[None, :]
    cosine = jnp.concatenate([jnp.cos(angles), jnp.cos(angles)], axis=1)
    sine_tab = jnp.concatenate([jnp.sin(angles), jnp.sin(angles)], axis=1)
    return (cosine, sine_tab)


def rotate(field, cosine, sine_tab):
    halves = HEAD_SIZE // 2
    turned = jnp.concatenate([-field[..., halves:], field[..., :halves]], axis=-1)
    return field * cosine[:, None, :] + turned * sine_tab[:, None, :]


def turn_matrix(cols):
    halves = HEAD_SIZE // 2
    c_in = jnp.arange(cols, dtype=jnp.int32)[:, None]
    c_out = jnp.arange(cols, dtype=jnp.int32)[None, :]
    local = c_out % HEAD_SIZE
    same_head = (c_in // HEAD_SIZE) == (c_out // HEAD_SIZE)
    low = same_head & (local < halves) & (c_in % HEAD_SIZE == local + halves)
    high = same_head & (local >= halves) & (c_in % HEAD_SIZE == local - halves)
    return jnp.where(low, -1.0, jnp.where(high, 1.0, 0.0)).astype(jnp.bfloat16)


def rotate_flat(field, cosine, sine_tab, turn):
    heads = field.shape[1] // HEAD_SIZE
    turned = jnp.dot(field, turn, preferred_element_type=jnp.float32)
    cos_all = jnp.tile(cosine, (1, heads))
    sin_all = jnp.tile(sine_tab, (1, heads))
    return (field.astype(jnp.float32) * cos_all + turned * sin_all).astype(jnp.bfloat16)


ROW_BLOCK = 128


def attend_kernel(q_ref, kc_ref, vc_ref, kn_ref, vn_ref, qrank_ref, cache_ok_ref, krank_ref, o_ref):
    score_scale = 1.0 / math.sqrt(HEAD_SIZE)
    query = q_ref[...]
    cols = query.shape[1]
    col_head = lax.broadcasted_iota(jnp.int32, (1, cols), 1) // HEAD_SIZE
    cache_ok = cache_ok_ref[...] > 0
    new_ok = krank_ref[...] <= qrank_ref[...]
    contract = (((1,), (1,)), ((), ()))
    total = jnp.zeros(o_ref.shape, jnp.float32)
    for head in range(cols // HEAD_SIZE):
        chosen = col_head == head
        head_query = jnp.where(chosen, query, jnp.zeros_like(query))
        score_c = lax.dot_general(
            head_query, kc_ref[...], contract, preferred_element_type=jnp.float32
        ) * score_scale
        score_n = lax.dot_general(
            head_query, kn_ref[...], contract, preferred_element_type=jnp.float32
        ) * score_scale
        score_c = jnp.where(cache_ok, score_c, -1e30)
        score_n = jnp.where(new_ok, score_n, -1e30)
        top = jnp.maximum(
            jnp.max(score_c, axis=1, keepdims=True), jnp.max(score_n, axis=1, keepdims=True)
        )
        weight_c = jnp.exp(score_c - top)
        weight_n = jnp.exp(score_n - top)
        whole = jnp.sum(weight_c, axis=1, keepdims=True) + jnp.sum(weight_n, axis=1, keepdims=True)
        prob_c = (weight_c / whole).astype(jnp.bfloat16)
        prob_n = (weight_n / whole).astype(jnp.bfloat16)
        head_out = jnp.dot(prob_c, vc_ref[...], preferred_element_type=jnp.float32) + jnp.dot(
            prob_n, vn_ref[...], preferred_element_type=jnp.float32
        )
        head_out = head_out.astype(jnp.bfloat16).astype(jnp.float32)
        total = total + jnp.where(chosen, head_out, 0.0)
    o_ref[...] = total.astype(o_ref.dtype)


def attend_flat(query, cache_keys, cache_values, fresh_keys, fresh_values, q_rank, cache_ok, k_rank):
    rows, cols = query.shape
    span = cache_keys.shape[0]
    whole = lambda i: (0, 0)
    block = ROW_BLOCK if rows % ROW_BLOCK == 0 else rows
    return pl.pallas_call(
        attend_kernel,
        out_shape=jax.ShapeDtypeStruct((rows, cols), jnp.bfloat16),
        grid=(rows // block,),
        in_specs=[
            pl.BlockSpec((block, cols), lambda i: (i, 0)),
            pl.BlockSpec((span, cols), whole),
            pl.BlockSpec((span, cols), whole),
            pl.BlockSpec((rows, cols), whole),
            pl.BlockSpec((rows, cols), whole),
            pl.BlockSpec((block, 1), lambda i: (i, 0)),
            pl.BlockSpec((1, span), whole),
            pl.BlockSpec((1, rows), whole),
        ],
        out_specs=pl.BlockSpec((block, cols), lambda i: (i, 0)),
    )(query, cache_keys, cache_values, fresh_keys, fresh_values, q_rank, cache_ok, k_rank)


def on_device(
    qkv_rows,
    row_request,
    request_owner,
    cached_len,
    page_table,
    kv_pages,
    residual,
    out_weight,
    norm_gain,
):
    row_count = qkv_rows.shape[0]
    parts = qkv_rows.shape[1]
    head_cols = qkv_rows.shape[2]
    heads_here = head_cols // HEAD_SIZE
    devices = lax.axis_size("req")
    slot_cap = SLOT
    buffer_len = devices * slot_cap
    device_ids = jnp.arange(devices, dtype=jnp.int32)
    row_ids = jnp.arange(row_count, dtype=jnp.int32)

    owner_dev = request_owner[row_request]
    same_owner = owner_dev[:, None] == owner_dev[None, :]
    slot_in = jnp.sum((same_owner & (row_ids[None, :] < row_ids[:, None])).astype(jnp.int32), axis=1)
    sends_to = owner_dev[:, None] == device_ids[None, :]
    counts = jnp.sum(sends_to.astype(jnp.int32), axis=0)

    pick = (
        sends_to[None, :, :]
        & (slot_in[None, :, None] == jnp.arange(slot_cap, dtype=jnp.int32)[:, None, None])
    ).astype(jnp.bfloat16)
    slots = jnp.einsum(
        "jid,ipc->dpjc", pick, qkv_rows, preferred_element_type=jnp.float32
    ).astype(jnp.bfloat16)
    count_row = jnp.broadcast_to(counts.astype(jnp.bfloat16)[:, None, None], (devices, 1, head_cols))
    outgoing = jnp.concatenate(
        [slots.reshape(devices, slot_cap * parts, head_cols), count_row], axis=1
    )
    arrived = lax.all_to_all(outgoing, "req", split_axis=0, concat_axis=0, tiled=True)
    arrived_counts = arrived[:, slot_cap * parts, 0].astype(jnp.int32)

    length = cached_len[0]
    pool_pages = kv_pages[page_table[0]]
    cache_span = pool_pages.shape[0] * pool_pages.shape[2]
    cache_keys = pool_pages[:, 0].reshape(cache_span, head_cols)
    cache_values = pool_pages[:, 1].reshape(cache_span, head_cols)
    live_slot = (jnp.arange(slot_cap, dtype=jnp.int32)[None, :] < arrived_counts[:, None]).reshape(
        buffer_len
    )
    live_int = live_slot.astype(jnp.int32)
    new_rank = jnp.cumsum(live_int) - live_int
    cosine, sine_tab = rope_tables(length + new_rank)
    cache_ok = (jnp.arange(cache_span, dtype=jnp.int32) < length).astype(jnp.int32)[None, :]
    k_rank = jnp.where(live_slot, new_rank, jnp.int32(2**30))[None, :]
    q_rank = new_rank[:, None]
    part_rows = [
        arrived[:, p * slot_cap : (p + 1) * slot_cap].reshape(buffer_len, head_cols)
        for p in range(parts)
    ]
    turn = turn_matrix(head_cols)
    query = rotate_flat(part_rows[0], cosine, sine_tab, turn)
    fresh_keys = rotate_flat(part_rows[1], cosine, sine_tab, turn)
    result = attend_flat(
        query, cache_keys, cache_values, fresh_keys, part_rows[2], q_rank, cache_ok, k_rank
    )
    returned = lax.all_to_all(
        result.reshape(devices, slot_cap * parts, head_cols // parts),
        "req",
        split_axis=0,
        concat_axis=0,
        tiled=True,
    )
    target = owner_dev * slot_cap + slot_in
    attn_rows = returned.reshape(buffer_len, head_cols)[target]
    partial_sum = jnp.dot(attn_rows, out_weight, preferred_element_type=jnp.float32)
    mixed_cols = lax.psum_scatter(
        partial_sum.astype(jnp.bfloat16), "tp", scatter_dimension=1, tiled=True
    ).astype(jnp.float32)
    hidden = residual.astype(jnp.float32) + mixed_cols
    square_sum = lax.psum(jnp.sum(hidden * hidden, axis=1), "tp")
    inv_rms = lax.rsqrt(square_sum / D + EPS)
    normed = hidden * inv_rms[:, None] * norm_gain.astype(jnp.float32)[None, :]
    return (hidden.astype(jnp.bfloat16), normed.astype(jnp.bfloat16))


def solution(mesh):
    return jax.shard_map(
        on_device,
        mesh=mesh,
        in_specs=(
            P("req", None, "tp"),
            P("req"),
            P(),
            P("req"),
            P("req", None),
            P("req", None, None, "tp"),
            P("req", "tp"),
            P("tp", None),
            P("tp"),
        ),
        out_specs=(P("req", "tp"), P("req", "tp")),
        check_vma=False,
    )
```

```python
import math

import jax
import jax.numpy as jnp
from jax import lax
from jax.experimental import pallas as pl
from jax.experimental.pallas import tpu as pltpu
from jax.sharding import PartitionSpec as P

D = 3072
HEAD_SIZE = 96
SLOT = 5

ROPE_BASE = 10000.0
EPS = 1e-05


def rope_tables(position):
    halves = HEAD_SIZE // 2
    inverse = ROPE_BASE ** (-2.0 * jnp.arange(halves, dtype=jnp.float32) / HEAD_SIZE)
    angles = position.astype(jnp.float32)[:, None] * inverse[None, :]
    cosine = jnp.concatenate([jnp.cos(angles), jnp.cos(angles)], axis=1)
    sine_tab = jnp.concatenate([jnp.sin(angles), jnp.sin(angles)], axis=1)
    return (cosine, sine_tab)


def rotate(field, cosine, sine_tab):
    halves = HEAD_SIZE // 2
    turned = jnp.concatenate([-field[..., halves:], field[..., :halves]], axis=-1)
    return field * cosine[:, None, :] + turned * sine_tab[:, None, :]


def turn_matrix(cols):
    halves = HEAD_SIZE // 2
    c_in = jnp.arange(cols, dtype=jnp.int32)[:, None]
    c_out = jnp.arange(cols, dtype=jnp.int32)[None, :]
    local = c_out % HEAD_SIZE
    same_head = (c_in // HEAD_SIZE) == (c_out // HEAD_SIZE)
    low = same_head & (local < halves) & (c_in % HEAD_SIZE == local + halves)
    high = same_head & (local >= halves) & (c_in % HEAD_SIZE == local - halves)
    return jnp.where(low, -1.0, jnp.where(high, 1.0, 0.0)).astype(jnp.bfloat16)


def rotate_flat(field, cosine, sine_tab, turn):
    heads = field.shape[1] // HEAD_SIZE
    turned = jnp.dot(field, turn, preferred_element_type=jnp.float32)
    cos_all = jnp.tile(cosine, (1, heads))
    sin_all = jnp.tile(sine_tab, (1, heads))
    return (field.astype(jnp.float32) * cos_all + turned * sin_all).astype(jnp.bfloat16)


def turn_rows(field, cos_rows, sin_rows, turn):
    turned = jnp.dot(field, turn, preferred_element_type=jnp.float32)
    return (field.astype(jnp.float32) * cos_rows + turned * sin_rows).astype(jnp.bfloat16)


def attend_kernel(
    q_ref, kn_ref, vn_ref, kc_ref, vc_ref, cos_ref, sin_ref, turn_ref, qrank_ref, cache_ok_ref,
    krank_ref, o_ref, keys_ref,
):
    step = pl.program_id(0)
    block = q_ref.shape[0]

    @pl.when(step == 0)
    def _():
        keys_ref[...] = turn_rows(kn_ref[...], cos_ref[...], sin_ref[...], turn_ref[...])

    here = pl.ds(pl.multiple_of(step * block, block), block)
    query = turn_rows(q_ref[...], cos_ref[here, :], sin_ref[here, :], turn_ref[...])
    score_scale = 1.0 / math.sqrt(HEAD_SIZE)
    cols = query.shape[1]
    col_head = lax.broadcasted_iota(jnp.int32, (1, cols), 1) // HEAD_SIZE
    cache_ok = cache_ok_ref[...] > 0
    new_ok = krank_ref[...] <= qrank_ref[...]
    contract = (((1,), (1,)), ((), ()))
    total = jnp.zeros(o_ref.shape, jnp.float32)
    for head in range(cols // HEAD_SIZE):
        chosen = col_head == head
        head_query = jnp.where(chosen, query, jnp.zeros_like(query))
        score_c = lax.dot_general(
            head_query, kc_ref[...], contract, preferred_element_type=jnp.float32
        ) * score_scale
        score_n = lax.dot_general(
            head_query, keys_ref[...], contract, preferred_element_type=jnp.float32
        ) * score_scale
        score_c = jnp.where(cache_ok, score_c, -1e30)
        score_n = jnp.where(new_ok, score_n, -1e30)
        top = jnp.maximum(
            jnp.max(score_c, axis=1, keepdims=True), jnp.max(score_n, axis=1, keepdims=True)
        )
        weight_c = jnp.exp(score_c - top)
        weight_n = jnp.exp(score_n - top)
        whole = jnp.sum(weight_c, axis=1, keepdims=True) + jnp.sum(weight_n, axis=1, keepdims=True)
        prob_c = (weight_c / whole).astype(jnp.bfloat16)
        prob_n = (weight_n / whole).astype(jnp.bfloat16)
        head_out = jnp.dot(prob_c, vc_ref[...], preferred_element_type=jnp.float32) + jnp.dot(
            prob_n, vn_ref[...], preferred_element_type=jnp.float32
        )
        head_out = head_out.astype(jnp.bfloat16).astype(jnp.float32)
        total = total + jnp.where(chosen, head_out, 0.0)
    o_ref[...] = total.astype(o_ref.dtype)


def attend_slots(query, fresh_keys, fresh_values, cache_keys, cache_values, cos_all, sin_all, turn,
                 q_rank, cache_ok, k_rank, slot_cap):
    rows, cols = query.shape
    block = rows // slot_cap
    span = cache_keys.shape[0]
    whole = lambda i: (0, 0)
    return pl.pallas_call(
        attend_kernel,
        out_shape=jax.ShapeDtypeStruct((block, slot_cap * cols), jnp.bfloat16),
        grid=(slot_cap,),
        in_specs=[
            pl.BlockSpec((block, cols), lambda i: (i, 0)),
            pl.BlockSpec((rows, cols), whole),
            pl.BlockSpec((rows, cols), whole),
            pl.BlockSpec((span, cols), whole),
            pl.BlockSpec((span, cols), whole),
            pl.BlockSpec((rows, cols), whole),
            pl.BlockSpec((rows, cols), whole),
            pl.BlockSpec((cols, cols), whole),
            pl.BlockSpec((block, 1), lambda i: (i, 0)),
            pl.BlockSpec((1, span), whole),
            pl.BlockSpec((1, rows), whole),
        ],
        out_specs=pl.BlockSpec((block, cols), lambda i: (0, i)),
        scratch_shapes=[pltpu.VMEM((rows, cols), jnp.bfloat16)],
        compiler_params=pltpu.CompilerParams(dimension_semantics=("arbitrary",)),
    )(query, fresh_keys, fresh_values, cache_keys, cache_values, cos_all, sin_all, turn, q_rank,
      cache_ok, k_rank)


def on_device(
    qkv_rows,
    row_request,
    request_owner,
    cached_len,
    page_table,
    kv_pages,
    residual,
    out_weight,
    norm_gain,
):
    row_count = qkv_rows.shape[0]
    parts = qkv_rows.shape[1]
    head_cols = qkv_rows.shape[2]
    heads_here = head_cols // HEAD_SIZE
    devices = lax.axis_size("req")
    slot_cap = SLOT
    buffer_len = devices * slot_cap
    device_ids = jnp.arange(devices, dtype=jnp.int32)
    row_ids = jnp.arange(row_count, dtype=jnp.int32)

    owner_dev = request_owner[row_request]
    same_owner = owner_dev[:, None] == owner_dev[None, :]
    slot_in = jnp.sum((same_owner & (row_ids[None, :] < row_ids[:, None])).astype(jnp.int32), axis=1)
    sends_to = owner_dev[:, None] == device_ids[None, :]
    counts = jnp.sum(sends_to.astype(jnp.int32), axis=0)

    pick = (
        sends_to[None, :, :]
        & (slot_in[None, :, None] == jnp.arange(slot_cap, dtype=jnp.int32)[:, None, None])
    ).astype(jnp.bfloat16)
    slots = jnp.einsum(
        "jid,ipc->dpjc", pick, qkv_rows, preferred_element_type=jnp.float32
    ).astype(jnp.bfloat16)
    count_row = jnp.broadcast_to(counts.astype(jnp.bfloat16)[:, None, None], (devices, 1, head_cols))
    outgoing = jnp.concatenate(
        [slots.reshape(devices, slot_cap * parts, head_cols), count_row], axis=1
    )
    arrived = lax.all_to_all(outgoing, "req", split_axis=0, concat_axis=0, tiled=True)
    planes = arrived.transpose(1, 0, 2)
    arrived_counts = planes[slot_cap * parts, :, 0].astype(jnp.int32)

    length = cached_len[0]
    pool_pages = kv_pages[page_table[0]]
    cache_span = pool_pages.shape[0] * pool_pages.shape[2]
    cache_keys = pool_pages[:, 0].reshape(cache_span, head_cols)
    cache_values = pool_pages[:, 1].reshape(cache_span, head_cols)
    slot_of = jnp.arange(slot_cap, dtype=jnp.int32)[:, None]
    before = jnp.cumsum(arrived_counts) - arrived_counts
    live_slot = (slot_of < arrived_counts[None, :]).reshape(buffer_len)
    new_rank = (before[None, :] + slot_of).reshape(buffer_len)
    cosine, sine_tab = rope_tables(length + new_rank)
    cos_all = jnp.tile(cosine, (1, heads_here))
    sin_all = jnp.tile(sine_tab, (1, heads_here))
    cache_ok = (jnp.arange(cache_span, dtype=jnp.int32) < length).astype(jnp.int32)[None, :]
    k_rank = jnp.where(live_slot, new_rank, jnp.int32(2**30))[None, :]
    q_rank = new_rank[:, None]
    part_rows = [
        planes[p * slot_cap : (p + 1) * slot_cap].reshape(buffer_len, head_cols)
        for p in range(parts)
    ]
    result = attend_slots(
        part_rows[0], part_rows[1], part_rows[2], cache_keys, cache_values, cos_all, sin_all,
        turn_matrix(head_cols), q_rank, cache_ok, k_rank, slot_cap,
    )
    returned = lax.all_to_all(
        result.reshape(devices, slot_cap * parts, head_cols // parts),
        "req",
        split_axis=0,
        concat_axis=0,
        tiled=True,
    )
    target = owner_dev * slot_cap + slot_in
    attn_rows = returned.reshape(buffer_len, head_cols)[target]
    partial_sum = jnp.dot(attn_rows, out_weight, preferred_element_type=jnp.float32)
    mixed_cols = lax.psum_scatter(
        partial_sum.astype(jnp.bfloat16), "tp", scatter_dimension=1, tiled=True
    ).astype(jnp.float32)
    hidden = residual.astype(jnp.float32) + mixed_cols
    square_sum = lax.psum(jnp.sum(hidden * hidden, axis=1), "tp")
    inv_rms = lax.rsqrt(square_sum / D + EPS)
    normed = hidden * inv_rms[:, None] * norm_gain.astype(jnp.float32)[None, :]
    return (hidden.astype(jnp.bfloat16), normed.astype(jnp.bfloat16))


def solution(mesh):
    return jax.shard_map(
        on_device,
        mesh=mesh,
        in_specs=(
            P("req", None, "tp"),
            P("req"),
            P(),
            P("req"),
            P("req", None),
            P("req", None, None, "tp"),
            P("req", "tp"),
            P("tp", None),
            P("tp"),
        ),
        out_specs=(P("req", "tp"), P("req", "tp")),
        check_vma=False,
    )
```

```python
import math

import jax
import jax.numpy as jnp
from jax import lax
from jax.experimental import pallas as pl
from jax.experimental.pallas import tpu as pltpu
from jax.sharding import PartitionSpec as P

D = 3072
HEAD_SIZE = 96
SLOT = 5

ROPE_BASE = 10000.0
EPS = 1e-05


def rope_tables(position):
    halves = HEAD_SIZE // 2
    inverse = ROPE_BASE ** (-2.0 * jnp.arange(halves, dtype=jnp.float32) / HEAD_SIZE)
    angles = position.astype(jnp.float32)[:, None] * inverse[None, :]
    cosine = jnp.concatenate([jnp.cos(angles), jnp.cos(angles)], axis=1)
    sine_tab = jnp.concatenate([jnp.sin(angles), jnp.sin(angles)], axis=1)
    return (cosine, sine_tab)


def rotate(field, cosine, sine_tab):
    halves = HEAD_SIZE // 2
    turned = jnp.concatenate([-field[..., halves:], field[..., :halves]], axis=-1)
    return field * cosine[:, None, :] + turned * sine_tab[:, None, :]


def turn_matrix(cols):
    halves = HEAD_SIZE // 2
    c_in = jnp.arange(cols, dtype=jnp.int32)[:, None]
    c_out = jnp.arange(cols, dtype=jnp.int32)[None, :]
    local = c_out % HEAD_SIZE
    same_head = (c_in // HEAD_SIZE) == (c_out // HEAD_SIZE)
    low = same_head & (local < halves) & (c_in % HEAD_SIZE == local + halves)
    high = same_head & (local >= halves) & (c_in % HEAD_SIZE == local - halves)
    return jnp.where(low, -1.0, jnp.where(high, 1.0, 0.0)).astype(jnp.bfloat16)


def rotate_flat(field, cosine, sine_tab, turn):
    heads = field.shape[1] // HEAD_SIZE
    turned = jnp.dot(field, turn, preferred_element_type=jnp.float32)
    cos_all = jnp.tile(cosine, (1, heads))
    sin_all = jnp.tile(sine_tab, (1, heads))
    return (field.astype(jnp.float32) * cos_all + turned * sin_all).astype(jnp.bfloat16)


def turn_rows(field, cos_rows, sin_rows, turn):
    turned = jnp.dot(field, turn, preferred_element_type=jnp.float32)
    return (field.astype(jnp.float32) * cos_rows + turned * sin_rows).astype(jnp.bfloat16)


def attend_kernel(
    q_ref, kn_ref, vn_ref, kc_ref, vc_ref, cos_ref, sin_ref, turn_ref, qrank_ref, cache_ok_ref,
    krank_ref, o_ref, keys_ref,
):
    step = pl.program_id(0)
    block = q_ref.shape[0]

    @pl.when(step == 0)
    def _():
        keys_ref[...] = turn_rows(kn_ref[...], cos_ref[...], sin_ref[...], turn_ref[...])

    here = pl.ds(pl.multiple_of(step * block, block), block)
    query = turn_rows(q_ref[...], cos_ref[here, :], sin_ref[here, :], turn_ref[...])
    score_scale = 1.0 / math.sqrt(HEAD_SIZE)
    cols = query.shape[1]
    col_head = lax.broadcasted_iota(jnp.int32, (1, cols), 1) // HEAD_SIZE
    cache_ok = cache_ok_ref[...] > 0
    new_ok = krank_ref[...] <= qrank_ref[...]
    contract = (((1,), (1,)), ((), ()))
    total = jnp.zeros(o_ref.shape, jnp.float32)
    for head in range(cols // HEAD_SIZE):
        chosen = col_head == head
        head_query = jnp.where(chosen, query, jnp.zeros_like(query))
        score_c = lax.dot_general(
            head_query, kc_ref[...], contract, preferred_element_type=jnp.float32
        ) * score_scale
        score_n = lax.dot_general(
            head_query, keys_ref[...], contract, preferred_element_type=jnp.float32
        ) * score_scale
        score_c = jnp.where(cache_ok, score_c, -1e30)
        score_n = jnp.where(new_ok, score_n, -1e30)
        top = jnp.maximum(
            jnp.max(score_c, axis=1, keepdims=True), jnp.max(score_n, axis=1, keepdims=True)
        )
        weight_c = jnp.exp(score_c - top)
        weight_n = jnp.exp(score_n - top)
        whole = jnp.sum(weight_c, axis=1, keepdims=True) + jnp.sum(weight_n, axis=1, keepdims=True)
        prob_c = (weight_c / whole).astype(jnp.bfloat16)
        prob_n = (weight_n / whole).astype(jnp.bfloat16)
        head_out = jnp.dot(prob_c, vc_ref[...], preferred_element_type=jnp.float32) + jnp.dot(
            prob_n, vn_ref[...], preferred_element_type=jnp.float32
        )
        head_out = head_out.astype(jnp.bfloat16).astype(jnp.float32)
        total = total + jnp.where(chosen, head_out, 0.0)
    o_ref[...] = total.astype(o_ref.dtype)


def attend_slots(query, fresh_keys, fresh_values, cache_keys, cache_values, cos_all, sin_all, turn,
                 q_rank, cache_ok, k_rank, slot_cap):
    rows, cols = query.shape
    block = rows // slot_cap
    span = cache_keys.shape[0]
    whole = lambda i: (0, 0)
    return pl.pallas_call(
        attend_kernel,
        out_shape=jax.ShapeDtypeStruct((block, slot_cap * cols), jnp.bfloat16),
        grid=(slot_cap,),
        in_specs=[
            pl.BlockSpec((block, cols), lambda i: (i, 0)),
            pl.BlockSpec((rows, cols), whole),
            pl.BlockSpec((rows, cols), whole),
            pl.BlockSpec((span, cols), whole),
            pl.BlockSpec((span, cols), whole),
            pl.BlockSpec((rows, cols), whole),
            pl.BlockSpec((rows, cols), whole),
            pl.BlockSpec((cols, cols), whole),
            pl.BlockSpec((block, 1), lambda i: (i, 0)),
            pl.BlockSpec((1, span), whole),
            pl.BlockSpec((1, rows), whole),
        ],
        out_specs=pl.BlockSpec((block, cols), lambda i: (0, i)),
        scratch_shapes=[pltpu.VMEM((rows, cols), jnp.bfloat16)],
        compiler_params=pltpu.CompilerParams(dimension_semantics=("arbitrary",)),
    )(query, fresh_keys, fresh_values, cache_keys, cache_values, cos_all, sin_all, turn, q_rank,
      cache_ok, k_rank)


def on_device(
    qkv_rows,
    row_request,
    request_owner,
    cached_len,
    page_table,
    kv_pages,
    residual,
    out_weight,
    norm_gain,
):
    row_count = qkv_rows.shape[0]
    parts = qkv_rows.shape[1]
    head_cols = qkv_rows.shape[2]
    heads_here = head_cols // HEAD_SIZE
    devices = lax.axis_size("req")
    slot_cap = SLOT
    buffer_len = devices * slot_cap
    device_ids = jnp.arange(devices, dtype=jnp.int32)
    row_ids = jnp.arange(row_count, dtype=jnp.int32)

    weight_cols = lax.all_to_all(out_weight, "tp", split_axis=1, concat_axis=0, tiled=True)
    owner_dev = request_owner[row_request]
    same_owner = owner_dev[:, None] == owner_dev[None, :]
    slot_in = jnp.sum((same_owner & (row_ids[None, :] < row_ids[:, None])).astype(jnp.int32), axis=1)
    sends_to = owner_dev[:, None] == device_ids[None, :]
    counts = jnp.sum(sends_to.astype(jnp.int32), axis=0)

    pick = (
        sends_to[None, :, :]
        & (slot_in[None, :, None] == jnp.arange(slot_cap, dtype=jnp.int32)[:, None, None])
    ).astype(jnp.bfloat16)
    slots = jnp.einsum(
        "jid,ipc->dpjc", pick, qkv_rows, preferred_element_type=jnp.float32
    ).astype(jnp.bfloat16)
    count_row = jnp.broadcast_to(counts.astype(jnp.bfloat16)[:, None, None], (devices, 1, head_cols))
    outgoing = jnp.concatenate(
        [slots.reshape(devices, slot_cap * parts, head_cols), count_row], axis=1
    )
    arrived = lax.all_to_all(outgoing, "req", split_axis=0, concat_axis=0, tiled=True)
    planes = arrived.transpose(1, 0, 2)
    arrived_counts = planes[slot_cap * parts, :, 0].astype(jnp.int32)

    length = cached_len[0]
    pool_pages = kv_pages[page_table[0]]
    cache_span = pool_pages.shape[0] * pool_pages.shape[2]
    cache_keys = pool_pages[:, 0].reshape(cache_span, head_cols)
    cache_values = pool_pages[:, 1].reshape(cache_span, head_cols)
    slot_of = jnp.arange(slot_cap, dtype=jnp.int32)[:, None]
    before = jnp.cumsum(arrived_counts) - arrived_counts
    live_slot = (slot_of < arrived_counts[None, :]).reshape(buffer_len)
    new_rank = (before[None, :] + slot_of).reshape(buffer_len)
    cosine, sine_tab = rope_tables(length + new_rank)
    cos_all = jnp.tile(cosine, (1, heads_here))
    sin_all = jnp.tile(sine_tab, (1, heads_here))
    cache_ok = (jnp.arange(cache_span, dtype=jnp.int32) < length).astype(jnp.int32)[None, :]
    k_rank = jnp.where(live_slot, new_rank, jnp.int32(2**30))[None, :]
    q_rank = new_rank[:, None]
    part_rows = [
        planes[p * slot_cap : (p + 1) * slot_cap].reshape(buffer_len, head_cols)
        for p in range(parts)
    ]
    result = attend_slots(
        part_rows[0], part_rows[1], part_rows[2], cache_keys, cache_values, cos_all, sin_all,
        turn_matrix(head_cols), q_rank, cache_ok, k_rank, slot_cap,
    )
    returned = lax.all_to_all(
        result.reshape(devices, slot_cap * parts, head_cols // parts),
        "req",
        split_axis=0,
        concat_axis=0,
        tiled=True,
    )
    target = owner_dev * slot_cap + slot_in
    attn_rows = returned.reshape(buffer_len, head_cols)[target]
    attn_all = lax.all_gather(attn_rows, "tp", axis=1, tiled=True)
    mixed_cols = jnp.dot(attn_all, weight_cols, preferred_element_type=jnp.float32)
    hidden = residual.astype(jnp.float32) + mixed_cols
    square_sum = lax.psum(jnp.sum(hidden * hidden, axis=1), "tp")
    inv_rms = lax.rsqrt(square_sum / D + EPS)
    normed = hidden * inv_rms[:, None] * norm_gain.astype(jnp.float32)[None, :]
    return (hidden.astype(jnp.bfloat16), normed.astype(jnp.bfloat16))


def solution(mesh):
    return jax.shard_map(
        on_device,
        mesh=mesh,
        in_specs=(
            P("req", None, "tp"),
            P("req"),
            P(),
            P("req"),
            P("req", None),
            P("req", None, None, "tp"),
            P("req", "tp"),
            P("tp", None),
            P("tp"),
        ),
        out_specs=(P("req", "tp"), P("req", "tp")),
        check_vma=False,
    )
```

```python
import math

import jax
import jax.numpy as jnp
from jax import lax
from jax.experimental import pallas as pl
from jax.experimental.pallas import tpu as pltpu
from jax.sharding import PartitionSpec as P

D = 3072
HEAD_SIZE = 96
SLOT = 5

ROPE_BASE = 10000.0
EPS = 1e-05


def rope_tables(position):
    halves = HEAD_SIZE // 2
    inverse = ROPE_BASE ** (-2.0 * jnp.arange(halves, dtype=jnp.float32) / HEAD_SIZE)
    angles = position.astype(jnp.float32)[:, None] * inverse[None, :]
    cosine = jnp.concatenate([jnp.cos(angles), jnp.cos(angles)], axis=1)
    sine_tab = jnp.concatenate([jnp.sin(angles), jnp.sin(angles)], axis=1)
    return (cosine, sine_tab)


def rotate(field, cosine, sine_tab):
    halves = HEAD_SIZE // 2
    turned = jnp.concatenate([-field[..., halves:], field[..., :halves]], axis=-1)
    return field * cosine[:, None, :] + turned * sine_tab[:, None, :]


def turn_matrix(cols):
    halves = HEAD_SIZE // 2
    c_in = jnp.arange(cols, dtype=jnp.int32)[:, None]
    c_out = jnp.arange(cols, dtype=jnp.int32)[None, :]
    local = c_out % HEAD_SIZE
    same_head = (c_in // HEAD_SIZE) == (c_out // HEAD_SIZE)
    low = same_head & (local < halves) & (c_in % HEAD_SIZE == local + halves)
    high = same_head & (local >= halves) & (c_in % HEAD_SIZE == local - halves)
    return jnp.where(low, -1.0, jnp.where(high, 1.0, 0.0)).astype(jnp.bfloat16)


def rotate_flat(field, cosine, sine_tab, turn):
    heads = field.shape[1] // HEAD_SIZE
    turned = jnp.dot(field, turn, preferred_element_type=jnp.float32)
    cos_all = jnp.tile(cosine, (1, heads))
    sin_all = jnp.tile(sine_tab, (1, heads))
    return (field.astype(jnp.float32) * cos_all + turned * sin_all).astype(jnp.bfloat16)


def turn_rows(field, cos_rows, sin_rows, turn):
    turned = jnp.dot(field, turn, preferred_element_type=jnp.float32)
    return (field.astype(jnp.float32) * cos_rows + turned * sin_rows).astype(jnp.bfloat16)


def attend_kernel(
    q_ref, kn_ref, vn_ref, kc_ref, vc_ref, cos_ref, sin_ref, turn_ref, qrank_ref, cache_ok_ref,
    krank_ref, o_ref, keys_ref,
):
    step = pl.program_id(0)
    block = q_ref.shape[0]

    @pl.when(step == 0)
    def _():
        keys_ref[...] = turn_rows(kn_ref[...], cos_ref[...], sin_ref[...], turn_ref[...])

    here = pl.ds(pl.multiple_of(step * block, block), block)
    query = turn_rows(q_ref[...], cos_ref[here, :], sin_ref[here, :], turn_ref[...])
    score_scale = 1.0 / math.sqrt(HEAD_SIZE)
    cols = query.shape[1]
    col_head = lax.broadcasted_iota(jnp.int32, (1, cols), 1) // HEAD_SIZE
    cache_ok = cache_ok_ref[...] > 0
    new_ok = krank_ref[...] <= qrank_ref[...]
    contract = (((1,), (1,)), ((), ()))
    total = jnp.zeros(o_ref.shape, jnp.float32)
    for head in range(cols // HEAD_SIZE):
        chosen = col_head == head
        head_query = jnp.where(chosen, query, jnp.zeros_like(query))
        score_c = lax.dot_general(
            head_query, kc_ref[...], contract, preferred_element_type=jnp.float32
        ) * score_scale
        score_n = lax.dot_general(
            head_query, keys_ref[...], contract, preferred_element_type=jnp.float32
        ) * score_scale
        score_c = jnp.where(cache_ok, score_c, -1e30)
        score_n = jnp.where(new_ok, score_n, -1e30)
        top = jnp.maximum(
            jnp.max(score_c, axis=1, keepdims=True), jnp.max(score_n, axis=1, keepdims=True)
        )
        weight_c = jnp.exp(score_c - top)
        weight_n = jnp.exp(score_n - top)
        whole = jnp.sum(weight_c, axis=1, keepdims=True) + jnp.sum(weight_n, axis=1, keepdims=True)
        prob_c = (weight_c / whole).astype(jnp.bfloat16)
        prob_n = (weight_n / whole).astype(jnp.bfloat16)
        head_out = jnp.dot(prob_c, vc_ref[...], preferred_element_type=jnp.float32) + jnp.dot(
            prob_n, vn_ref[...], preferred_element_type=jnp.float32
        )
        head_out = head_out.astype(jnp.bfloat16).astype(jnp.float32)
        total = total + jnp.where(chosen, head_out, 0.0)
    o_ref[...] = total.astype(o_ref.dtype)


def attend_slots(query, fresh_keys, fresh_values, cache_keys, cache_values, cos_all, sin_all, turn,
                 q_rank, cache_ok, k_rank, slot_cap):
    rows, cols = query.shape
    block = rows // slot_cap
    span = cache_keys.shape[0]
    whole = lambda i: (0, 0)
    return pl.pallas_call(
        attend_kernel,
        out_shape=jax.ShapeDtypeStruct((block, slot_cap * cols), jnp.bfloat16),
        grid=(slot_cap,),
        in_specs=[
            pl.BlockSpec((block, cols), lambda i: (i, 0)),
            pl.BlockSpec((rows, cols), whole),
            pl.BlockSpec((rows, cols), whole),
            pl.BlockSpec((span, cols), whole),
            pl.BlockSpec((span, cols), whole),
            pl.BlockSpec((rows, cols), whole),
            pl.BlockSpec((rows, cols), whole),
            pl.BlockSpec((cols, cols), whole),
            pl.BlockSpec((block, 1), lambda i: (i, 0)),
            pl.BlockSpec((1, span), whole),
            pl.BlockSpec((1, rows), whole),
        ],
        out_specs=pl.BlockSpec((block, cols), lambda i: (0, i)),
        scratch_shapes=[pltpu.VMEM((rows, cols), jnp.bfloat16)],
        compiler_params=pltpu.CompilerParams(dimension_semantics=("arbitrary",)),
    )(query, fresh_keys, fresh_values, cache_keys, cache_values, cos_all, sin_all, turn, q_rank,
      cache_ok, k_rank)


def on_device(
    qkv_rows,
    row_request,
    request_owner,
    cached_len,
    page_table,
    kv_pages,
    residual,
    out_weight,
    norm_gain,
):
    row_count = qkv_rows.shape[0]
    parts = qkv_rows.shape[1]
    head_cols = qkv_rows.shape[2]
    heads_here = head_cols // HEAD_SIZE
    devices = lax.axis_size("req")
    slot_cap = SLOT
    buffer_len = devices * slot_cap
    device_ids = jnp.arange(devices, dtype=jnp.int32)
    row_ids = jnp.arange(row_count, dtype=jnp.int32)

    weight_cols = lax.all_to_all(out_weight, "tp", split_axis=1, concat_axis=0, tiled=True)
    owner_dev = request_owner[row_request]
    same_owner = owner_dev[:, None] == owner_dev[None, :]
    slot_in = jnp.sum((same_owner & (row_ids[None, :] < row_ids[:, None])).astype(jnp.int32), axis=1)
    sends_to = owner_dev[:, None] == device_ids[None, :]
    counts = jnp.sum(sends_to.astype(jnp.int32), axis=0)

    pick = (
        sends_to[None, :, :]
        & (slot_in[None, :, None] == jnp.arange(slot_cap, dtype=jnp.int32)[:, None, None])
    ).astype(jnp.bfloat16)
    slots = jnp.einsum(
        "jid,ipc->dpjc", pick, qkv_rows, preferred_element_type=jnp.float32
    ).astype(jnp.bfloat16)
    count_row = jnp.broadcast_to(counts.astype(jnp.bfloat16)[:, None, None], (devices, 1, head_cols))
    outgoing = jnp.concatenate(
        [slots.reshape(devices, slot_cap * parts, head_cols), count_row], axis=1
    )
    arrived = lax.all_to_all(outgoing, "req", split_axis=0, concat_axis=0, tiled=True)
    planes = arrived.transpose(1, 0, 2)
    arrived_counts = planes[slot_cap * parts, :, 0].astype(jnp.int32)

    length = cached_len[0]
    pool_pages = kv_pages[page_table[0]]
    cache_span = pool_pages.shape[0] * pool_pages.shape[2]
    cache_keys = pool_pages[:, 0].reshape(cache_span, head_cols)
    cache_values = pool_pages[:, 1].reshape(cache_span, head_cols)
    slot_of = jnp.arange(slot_cap, dtype=jnp.int32)[:, None]
    before = jnp.cumsum(arrived_counts) - arrived_counts
    live_slot = (slot_of < arrived_counts[None, :]).reshape(buffer_len)
    new_rank = (before[None, :] + slot_of).reshape(buffer_len)
    cosine, sine_tab = rope_tables(length + new_rank)
    cos_all = jnp.tile(cosine, (1, heads_here))
    sin_all = jnp.tile(sine_tab, (1, heads_here))
    cache_ok = (jnp.arange(cache_span, dtype=jnp.int32) < length).astype(jnp.int32)[None, :]
    k_rank = jnp.where(live_slot, new_rank, jnp.int32(2**30))[None, :]
    q_rank = new_rank[:, None]
    part_rows = [
        planes[p * slot_cap : (p + 1) * slot_cap].reshape(buffer_len, head_cols)
        for p in range(parts)
    ]
    result = attend_slots(
        part_rows[0], part_rows[1], part_rows[2], cache_keys, cache_values, cos_all, sin_all,
        turn_matrix(head_cols), q_rank, cache_ok, k_rank, slot_cap,
    )
    returned = lax.all_to_all(
        result.reshape(devices, slot_cap * parts, head_cols // parts),
        "req",
        split_axis=0,
        concat_axis=0,
        tiled=True,
    )
    target = owner_dev * slot_cap + slot_in
    attn_rows = returned.reshape(buffer_len, head_cols)[target]
    tp_size = lax.axis_size("tp")
    attn_all = lax.all_to_all(
        jnp.broadcast_to(attn_rows[None], (tp_size,) + attn_rows.shape), "tp", 0, 0, tiled=True
    )
    mixed_cols = jnp.einsum(
        "tmc,tcn->mn",
        attn_all,
        weight_cols.reshape(attn_all.shape[0], head_cols, -1),
        preferred_element_type=jnp.float32,
    )
    hidden = residual.astype(jnp.float32) + mixed_cols
    square_part = jnp.sum(hidden * hidden, axis=1)
    square_sum = jnp.sum(
        lax.all_to_all(
            jnp.broadcast_to(square_part[None], (tp_size,) + square_part.shape), "tp", 0, 0, tiled=True
        ),
        axis=0,
    )
    inv_rms = lax.rsqrt(square_sum / D + EPS)
    normed = hidden * inv_rms[:, None] * norm_gain.astype(jnp.float32)[None, :]
    return (hidden.astype(jnp.bfloat16), normed.astype(jnp.bfloat16))


def solution(mesh):
    return jax.shard_map(
        on_device,
        mesh=mesh,
        in_specs=(
            P("req", None, "tp"),
            P("req"),
            P(),
            P("req"),
            P("req", None),
            P("req", None, None, "tp"),
            P("req", "tp"),
            P("tp", None),
            P("tp"),
        ),
        out_specs=(P("req", "tp"), P("req", "tp")),
        check_vma=False,
    )
```

```python
import math

import jax
import jax.numpy as jnp
from jax import lax
from jax.experimental import pallas as pl
from jax.experimental.pallas import tpu as pltpu
from jax.sharding import PartitionSpec as P

D = 3072
HEAD_SIZE = 96
SLOT = 5

ROPE_BASE = 10000.0
EPS = 1e-05


def rope_tables(position):
    halves = HEAD_SIZE // 2
    inverse = ROPE_BASE ** (-2.0 * jnp.arange(halves, dtype=jnp.float32) / HEAD_SIZE)
    angles = position.astype(jnp.float32)[:, None] * inverse[None, :]
    cosine = jnp.concatenate([jnp.cos(angles), jnp.cos(angles)], axis=1)
    sine_tab = jnp.concatenate([jnp.sin(angles), jnp.sin(angles)], axis=1)
    return (cosine, sine_tab)


def rotate(field, cosine, sine_tab):
    halves = HEAD_SIZE // 2
    turned = jnp.concatenate([-field[..., halves:], field[..., :halves]], axis=-1)
    return field * cosine[:, None, :] + turned * sine_tab[:, None, :]


def turn_matrix(cols):
    halves = HEAD_SIZE // 2
    c_in = jnp.arange(cols, dtype=jnp.int32)[:, None]
    c_out = jnp.arange(cols, dtype=jnp.int32)[None, :]
    local = c_out % HEAD_SIZE
    same_head = (c_in // HEAD_SIZE) == (c_out // HEAD_SIZE)
    low = same_head & (local < halves) & (c_in % HEAD_SIZE == local + halves)
    high = same_head & (local >= halves) & (c_in % HEAD_SIZE == local - halves)
    return jnp.where(low, -1.0, jnp.where(high, 1.0, 0.0)).astype(jnp.bfloat16)


def rotate_flat(field, cosine, sine_tab, turn):
    heads = field.shape[1] // HEAD_SIZE
    turned = jnp.dot(field, turn, preferred_element_type=jnp.float32)
    cos_all = jnp.tile(cosine, (1, heads))
    sin_all = jnp.tile(sine_tab, (1, heads))
    return (field.astype(jnp.float32) * cos_all + turned * sin_all).astype(jnp.bfloat16)


def turn_rows(field, cos_rows, sin_rows, turn):
    turned = jnp.dot(field, turn, preferred_element_type=jnp.float32)
    return (field.astype(jnp.float32) * cos_rows + turned * sin_rows).astype(jnp.bfloat16)


def attend_kernel(
    q_ref, kn_ref, vn_ref, kc_ref, vc_ref, cos_ref, sin_ref, turn_ref, qrank_ref, cache_ok_ref,
    krank_ref, o_ref, keys_ref,
):
    step = pl.program_id(0)
    block = q_ref.shape[0]

    @pl.when(step == 0)
    def _():
        keys_ref[...] = turn_rows(kn_ref[...], cos_ref[...], sin_ref[...], turn_ref[...])

    here = pl.ds(pl.multiple_of(step * block, block), block)
    query = turn_rows(q_ref[...], cos_ref[here, :], sin_ref[here, :], turn_ref[...])
    score_scale = 1.0 / math.sqrt(HEAD_SIZE)
    cols = query.shape[1]
    col_head = lax.broadcasted_iota(jnp.int32, (1, cols), 1) // HEAD_SIZE
    cache_ok = cache_ok_ref[...] > 0
    new_ok = krank_ref[...] <= qrank_ref[...]
    contract = (((1,), (1,)), ((), ()))
    total = jnp.zeros(o_ref.shape, jnp.float32)
    for head in range(cols // HEAD_SIZE):
        chosen = col_head == head
        head_query = jnp.where(chosen, query, jnp.zeros_like(query))
        score_c = lax.dot_general(
            head_query, kc_ref[...], contract, preferred_element_type=jnp.float32
        ) * score_scale
        score_n = lax.dot_general(
            head_query, keys_ref[...], contract, preferred_element_type=jnp.float32
        ) * score_scale
        score_c = jnp.where(cache_ok, score_c, -1e30)
        score_n = jnp.where(new_ok, score_n, -1e30)
        top = jnp.maximum(
            jnp.max(score_c, axis=1, keepdims=True), jnp.max(score_n, axis=1, keepdims=True)
        )
        weight_c = jnp.exp(score_c - top)
        weight_n = jnp.exp(score_n - top)
        whole = jnp.sum(weight_c, axis=1, keepdims=True) + jnp.sum(weight_n, axis=1, keepdims=True)
        prob_c = (weight_c / whole).astype(jnp.bfloat16)
        prob_n = (weight_n / whole).astype(jnp.bfloat16)
        head_out = jnp.dot(prob_c, vc_ref[...], preferred_element_type=jnp.float32) + jnp.dot(
            prob_n, vn_ref[...], preferred_element_type=jnp.float32
        )
        head_out = head_out.astype(jnp.bfloat16).astype(jnp.float32)
        total = total + jnp.where(chosen, head_out, 0.0)
    o_ref[...] = total.astype(o_ref.dtype)


def attend_slots(query, fresh_keys, fresh_values, cache_keys, cache_values, cos_all, sin_all, turn,
                 q_rank, cache_ok, k_rank, slot_cap):
    rows, cols = query.shape
    block = rows // slot_cap
    span = cache_keys.shape[0]
    whole = lambda i: (0, 0)
    return pl.pallas_call(
        attend_kernel,
        out_shape=jax.ShapeDtypeStruct((block, slot_cap * cols), jnp.bfloat16),
        grid=(slot_cap,),
        in_specs=[
            pl.BlockSpec((block, cols), lambda i: (i, 0)),
            pl.BlockSpec((rows, cols), whole),
            pl.BlockSpec((rows, cols), whole),
            pl.BlockSpec((span, cols), whole),
            pl.BlockSpec((span, cols), whole),
            pl.BlockSpec((rows, cols), whole),
            pl.BlockSpec((rows, cols), whole),
            pl.BlockSpec((cols, cols), whole),
            pl.BlockSpec((block, 1), lambda i: (i, 0)),
            pl.BlockSpec((1, span), whole),
            pl.BlockSpec((1, rows), whole),
        ],
        out_specs=pl.BlockSpec((block, cols), lambda i: (0, i)),
        scratch_shapes=[pltpu.VMEM((rows, cols), jnp.bfloat16)],
        compiler_params=pltpu.CompilerParams(dimension_semantics=("arbitrary",)),
    )(query, fresh_keys, fresh_values, cache_keys, cache_values, cos_all, sin_all, turn, q_rank,
      cache_ok, k_rank)


def tp_shift(x, k, tp_size):
    return lax.ppermute(x, "tp", perm=[(i, (i + k) % tp_size) for i in range(tp_size)])


def on_device(
    qkv_rows,
    row_request,
    request_owner,
    cached_len,
    page_table,
    kv_pages,
    residual,
    out_weight,
    norm_gain,
):
    row_count = qkv_rows.shape[0]
    parts = qkv_rows.shape[1]
    head_cols = qkv_rows.shape[2]
    heads_here = head_cols // HEAD_SIZE
    devices = lax.axis_size("req")
    slot_cap = SLOT
    buffer_len = devices * slot_cap
    device_ids = jnp.arange(devices, dtype=jnp.int32)
    row_ids = jnp.arange(row_count, dtype=jnp.int32)

    weight_cols = lax.all_to_all(out_weight, "tp", split_axis=1, concat_axis=0, tiled=True)
    owner_dev = request_owner[row_request]
    same_owner = owner_dev[:, None] == owner_dev[None, :]
    slot_in = jnp.sum((same_owner & (row_ids[None, :] < row_ids[:, None])).astype(jnp.int32), axis=1)
    sends_to = owner_dev[:, None] == device_ids[None, :]
    counts = jnp.sum(sends_to.astype(jnp.int32), axis=0)

    pick = (
        sends_to[None, :, :]
        & (slot_in[None, :, None] == jnp.arange(slot_cap, dtype=jnp.int32)[:, None, None])
    ).astype(jnp.bfloat16)
    slots = jnp.einsum(
        "jid,ipc->dpjc", pick, qkv_rows, preferred_element_type=jnp.float32
    ).astype(jnp.bfloat16)
    count_row = jnp.broadcast_to(counts.astype(jnp.bfloat16)[:, None, None], (devices, 1, head_cols))
    outgoing = jnp.concatenate(
        [slots.reshape(devices, slot_cap * parts, head_cols), count_row], axis=1
    )
    arrived = lax.all_to_all(outgoing, "req", split_axis=0, concat_axis=0, tiled=True)
    planes = arrived.transpose(1, 0, 2)
    arrived_counts = planes[slot_cap * parts, :, 0].astype(jnp.int32)

    length = cached_len[0]
    pool_pages = kv_pages[page_table[0]]
    cache_span = pool_pages.shape[0] * pool_pages.shape[2]
    cache_keys = pool_pages[:, 0].reshape(cache_span, head_cols)
    cache_values = pool_pages[:, 1].reshape(cache_span, head_cols)
    slot_of = jnp.arange(slot_cap, dtype=jnp.int32)[:, None]
    before = jnp.cumsum(arrived_counts) - arrived_counts
    live_slot = (slot_of < arrived_counts[None, :]).reshape(buffer_len)
    new_rank = (before[None, :] + slot_of).reshape(buffer_len)
    cosine, sine_tab = rope_tables(length + new_rank)
    cos_all = jnp.tile(cosine, (1, heads_here))
    sin_all = jnp.tile(sine_tab, (1, heads_here))
    cache_ok = (jnp.arange(cache_span, dtype=jnp.int32) < length).astype(jnp.int32)[None, :]
    k_rank = jnp.where(live_slot, new_rank, jnp.int32(2**30))[None, :]
    q_rank = new_rank[:, None]
    part_rows = [
        planes[p * slot_cap : (p + 1) * slot_cap].reshape(buffer_len, head_cols)
        for p in range(parts)
    ]
    result = attend_slots(
        part_rows[0], part_rows[1], part_rows[2], cache_keys, cache_values, cos_all, sin_all,
        turn_matrix(head_cols), q_rank, cache_ok, k_rank, slot_cap,
    )
    returned = lax.all_to_all(
        result.reshape(devices, slot_cap * parts, head_cols // parts),
        "req",
        split_axis=0,
        concat_axis=0,
        tiled=True,
    )
    target = owner_dev * slot_cap + slot_in
    attn_rows = returned.reshape(buffer_len, head_cols)[target]
    tp_size = lax.axis_size("tp")
    tp_here = lax.axis_index("tp")
    from_dev = (tp_here - jnp.arange(tp_size, dtype=jnp.int32)) % tp_size
    weight_blocks = jnp.take(weight_cols.reshape(tp_size, head_cols, -1), from_dev, axis=0)
    attn_all = jnp.stack([attn_rows] + [tp_shift(attn_rows, k, tp_size) for k in range(1, tp_size)])
    mixed_cols = jnp.einsum(
        "kmc,kcn->mn", attn_all, weight_blocks, preferred_element_type=jnp.float32
    )
    hidden = residual.astype(jnp.float32) + mixed_cols
    square_part = jnp.sum(hidden * hidden, axis=1)
    shifted = jnp.stack(
        [square_part] + [tp_shift(square_part, k, tp_size) for k in range(1, tp_size)]
    )
    by_source = jnp.take(shifted, (tp_here - jnp.arange(tp_size, dtype=jnp.int32)) % tp_size, axis=0)
    square_sum = by_source[0]
    for k in range(1, tp_size):
        square_sum = square_sum + by_source[k]
    inv_rms = lax.rsqrt(square_sum / D + EPS)
    normed = hidden * inv_rms[:, None] * norm_gain.astype(jnp.float32)[None, :]
    return (hidden.astype(jnp.bfloat16), normed.astype(jnp.bfloat16))


def solution(mesh):
    return jax.shard_map(
        on_device,
        mesh=mesh,
        in_specs=(
            P("req", None, "tp"),
            P("req"),
            P(),
            P("req"),
            P("req", None),
            P("req", None, None, "tp"),
            P("req", "tp"),
            P("tp", None),
            P("tp"),
        ),
        out_specs=(P("req", "tp"), P("req", "tp")),
        check_vma=False,
    )
```

```python
import math

import jax
import jax.numpy as jnp
from jax import lax
from jax.experimental import pallas as pl
from jax.experimental.pallas import tpu as pltpu
from jax.sharding import PartitionSpec as P

D = 3072
HEAD_SIZE = 96
SLOT = 5

ROPE_BASE = 10000.0
EPS = 1e-05


def rope_tables(position):
    halves = HEAD_SIZE // 2
    inverse = ROPE_BASE ** (-2.0 * jnp.arange(halves, dtype=jnp.float32) / HEAD_SIZE)
    angles = position.astype(jnp.float32)[:, None] * inverse[None, :]
    cosine = jnp.concatenate([jnp.cos(angles), jnp.cos(angles)], axis=1)
    sine_tab = jnp.concatenate([jnp.sin(angles), jnp.sin(angles)], axis=1)
    return (cosine, sine_tab)


def rotate(field, cosine, sine_tab):
    halves = HEAD_SIZE // 2
    turned = jnp.concatenate([-field[..., halves:], field[..., :halves]], axis=-1)
    return field * cosine[:, None, :] + turned * sine_tab[:, None, :]


def turn_matrix(cols):
    halves = HEAD_SIZE // 2
    c_in = jnp.arange(cols, dtype=jnp.int32)[:, None]
    c_out = jnp.arange(cols, dtype=jnp.int32)[None, :]
    local = c_out % HEAD_SIZE
    same_head = (c_in // HEAD_SIZE) == (c_out // HEAD_SIZE)
    low = same_head & (local < halves) & (c_in % HEAD_SIZE == local + halves)
    high = same_head & (local >= halves) & (c_in % HEAD_SIZE == local - halves)
    return jnp.where(low, -1.0, jnp.where(high, 1.0, 0.0)).astype(jnp.bfloat16)


def rotate_flat(field, cosine, sine_tab, turn):
    heads = field.shape[1] // HEAD_SIZE
    turned = jnp.dot(field, turn, preferred_element_type=jnp.float32)
    cos_all = jnp.tile(cosine, (1, heads))
    sin_all = jnp.tile(sine_tab, (1, heads))
    return (field.astype(jnp.float32) * cos_all + turned * sin_all).astype(jnp.bfloat16)


def turn_rows(field, positions, inverse, turn):
    angles = positions.astype(jnp.float32) * inverse
    turned = jnp.dot(field, turn, preferred_element_type=jnp.float32)
    return (field.astype(jnp.float32) * jnp.cos(angles) + turned * jnp.sin(angles)).astype(
        jnp.bfloat16
    )


def attend_kernel(
    q_ref, kn_ref, vn_ref, kc_ref, vc_ref, pos_ref, inv_ref, turn_ref, qrank_ref, cache_ok_ref,
    krank_ref, o_ref, keys_ref,
):
    step = pl.program_id(0)
    block = q_ref.shape[0]

    @pl.when(step == 0)
    def _():
        keys_ref[...] = turn_rows(kn_ref[...], pos_ref[...], inv_ref[...], turn_ref[...])

    here = pl.ds(pl.multiple_of(step * block, block), block)
    query = turn_rows(q_ref[...], pos_ref[here, :], inv_ref[...], turn_ref[...])
    score_scale = 1.0 / math.sqrt(HEAD_SIZE)
    cols = query.shape[1]
    col_head = lax.broadcasted_iota(jnp.int32, (1, cols), 1) // HEAD_SIZE
    cache_ok = cache_ok_ref[...] > 0
    new_ok = krank_ref[...] <= qrank_ref[...]
    contract = (((1,), (1,)), ((), ()))
    total = jnp.zeros(o_ref.shape, jnp.float32)
    for head in range(cols // HEAD_SIZE):
        chosen = col_head == head
        head_query = jnp.where(chosen, query, jnp.zeros_like(query))
        score_c = lax.dot_general(
            head_query, kc_ref[...], contract, preferred_element_type=jnp.float32
        ) * score_scale
        score_n = lax.dot_general(
            head_query, keys_ref[...], contract, preferred_element_type=jnp.float32
        ) * score_scale
        score_c = jnp.where(cache_ok, score_c, -1e30)
        score_n = jnp.where(new_ok, score_n, -1e30)
        top = jnp.maximum(
            jnp.max(score_c, axis=1, keepdims=True), jnp.max(score_n, axis=1, keepdims=True)
        )
        weight_c = jnp.exp(score_c - top)
        weight_n = jnp.exp(score_n - top)
        whole = jnp.sum(weight_c, axis=1, keepdims=True) + jnp.sum(weight_n, axis=1, keepdims=True)
        prob_c = (weight_c / whole).astype(jnp.bfloat16)
        prob_n = (weight_n / whole).astype(jnp.bfloat16)
        head_out = jnp.dot(prob_c, vc_ref[...], preferred_element_type=jnp.float32) + jnp.dot(
            prob_n, vn_ref[...], preferred_element_type=jnp.float32
        )
        head_out = head_out.astype(jnp.bfloat16).astype(jnp.float32)
        total = total + jnp.where(chosen, head_out, 0.0)
    o_ref[...] = total.astype(o_ref.dtype)


def attend_slots(query, fresh_keys, fresh_values, cache_keys, cache_values, positions, inverse, turn,
                 q_rank, cache_ok, k_rank, slot_cap):
    rows, cols = query.shape
    block = rows // slot_cap
    span = cache_keys.shape[0]
    whole = lambda i: (0, 0)
    return pl.pallas_call(
        attend_kernel,
        out_shape=jax.ShapeDtypeStruct((block, slot_cap * cols), jnp.bfloat16),
        grid=(slot_cap,),
        in_specs=[
            pl.BlockSpec((block, cols), lambda i: (i, 0)),
            pl.BlockSpec((rows, cols), whole),
            pl.BlockSpec((rows, cols), whole),
            pl.BlockSpec((span, cols), whole),
            pl.BlockSpec((span, cols), whole),
            pl.BlockSpec((rows, 1), whole),
            pl.BlockSpec((1, cols), whole),
            pl.BlockSpec((cols, cols), whole),
            pl.BlockSpec((block, 1), lambda i: (i, 0)),
            pl.BlockSpec((1, span), whole),
            pl.BlockSpec((1, rows), whole),
        ],
        out_specs=pl.BlockSpec((block, cols), lambda i: (0, i)),
        scratch_shapes=[pltpu.VMEM((rows, cols), jnp.bfloat16)],
        compiler_params=pltpu.CompilerParams(dimension_semantics=("arbitrary",)),
    )(query, fresh_keys, fresh_values, cache_keys, cache_values, positions, inverse, turn, q_rank,
      cache_ok, k_rank)


def on_device(
    qkv_rows,
    row_request,
    request_owner,
    cached_len,
    page_table,
    kv_pages,
    residual,
    out_weight,
    norm_gain,
):
    row_count = qkv_rows.shape[0]
    parts = qkv_rows.shape[1]
    head_cols = qkv_rows.shape[2]
    heads_here = head_cols // HEAD_SIZE
    devices = lax.axis_size("req")
    slot_cap = SLOT
    buffer_len = devices * slot_cap
    device_ids = jnp.arange(devices, dtype=jnp.int32)
    row_ids = jnp.arange(row_count, dtype=jnp.int32)

    weight_cols = lax.all_to_all(out_weight, "tp", split_axis=1, concat_axis=0, tiled=True)
    owner_dev = request_owner[row_request]
    same_owner = owner_dev[:, None] == owner_dev[None, :]
    slot_in = jnp.sum((same_owner & (row_ids[None, :] < row_ids[:, None])).astype(jnp.int32), axis=1)
    sends_to = owner_dev[:, None] == device_ids[None, :]
    counts = jnp.sum(sends_to.astype(jnp.int32), axis=0)

    pick = (
        sends_to[None, :, :]
        & (slot_in[None, :, None] == jnp.arange(slot_cap, dtype=jnp.int32)[:, None, None])
    ).astype(jnp.bfloat16)
    slots = jnp.einsum(
        "jid,ipc->dpjc", pick, qkv_rows, preferred_element_type=jnp.float32
    ).astype(jnp.bfloat16)
    count_row = jnp.broadcast_to(counts.astype(jnp.bfloat16)[:, None, None], (devices, 1, head_cols))
    outgoing = jnp.concatenate(
        [slots.reshape(devices, slot_cap * parts, head_cols), count_row], axis=1
    )
    arrived = lax.all_to_all(outgoing, "req", split_axis=0, concat_axis=0, tiled=True)
    planes = arrived.transpose(1, 0, 2)
    arrived_counts = planes[slot_cap * parts, :, 0].astype(jnp.int32)

    length = cached_len[0]
    pool_pages = kv_pages[page_table[0]]
    cache_span = pool_pages.shape[0] * pool_pages.shape[2]
    cache_keys = pool_pages[:, 0].reshape(cache_span, head_cols)
    cache_values = pool_pages[:, 1].reshape(cache_span, head_cols)
    slot_of = jnp.arange(slot_cap, dtype=jnp.int32)[:, None]
    before = jnp.cumsum(arrived_counts) - arrived_counts
    live_slot = (slot_of < arrived_counts[None, :]).reshape(buffer_len)
    new_rank = (before[None, :] + slot_of).reshape(buffer_len)
    positions = (length + new_rank)[:, None]
    halves = HEAD_SIZE // 2
    inverse = ROPE_BASE ** (-2.0 * jnp.arange(halves, dtype=jnp.float32) / HEAD_SIZE)
    inverse = jnp.tile(inverse, 2 * heads_here)[None, :]
    cache_ok = (jnp.arange(cache_span, dtype=jnp.int32) < length).astype(jnp.int32)[None, :]
    k_rank = jnp.where(live_slot, new_rank, jnp.int32(2**30))[None, :]
    q_rank = new_rank[:, None]
    part_rows = [
        planes[p * slot_cap : (p + 1) * slot_cap].reshape(buffer_len, head_cols)
        for p in range(parts)
    ]
    result = attend_slots(
        part_rows[0], part_rows[1], part_rows[2], cache_keys, cache_values, positions, inverse,
        turn_matrix(head_cols), q_rank, cache_ok, k_rank, slot_cap,
    )
    returned = lax.all_to_all(
        result.reshape(devices, slot_cap * parts, head_cols // parts),
        "req",
        split_axis=0,
        concat_axis=0,
        tiled=True,
    )
    target = owner_dev * slot_cap + slot_in
    attn_rows = returned.reshape(buffer_len, head_cols)[target]
    attn_all = lax.all_gather(attn_rows, "tp", axis=1, tiled=True)
    mixed_cols = jnp.dot(attn_all, weight_cols, preferred_element_type=jnp.float32)
    hidden = residual.astype(jnp.float32) + mixed_cols
    square_sum = lax.psum(jnp.sum(hidden * hidden, axis=1), "tp")
    inv_rms = lax.rsqrt(square_sum / D + EPS)
    normed = hidden * inv_rms[:, None] * norm_gain.astype(jnp.float32)[None, :]
    return (hidden.astype(jnp.bfloat16), normed.astype(jnp.bfloat16))


def solution(mesh):
    return jax.shard_map(
        on_device,
        mesh=mesh,
        in_specs=(
            P("req", None, "tp"),
            P("req"),
            P(),
            P("req"),
            P("req", None),
            P("req", None, None, "tp"),
            P("req", "tp"),
            P("tp", None),
            P("tp"),
        ),
        out_specs=(P("req", "tp"), P("req", "tp")),
        check_vma=False,
    )
```

```python
import math

import jax
import jax.numpy as jnp
from jax import lax
from jax.experimental import pallas as pl
from jax.experimental.pallas import tpu as pltpu
from jax.sharding import PartitionSpec as P

D = 3072
HEAD_SIZE = 96
SLOT = 5

ROPE_BASE = 10000.0
EPS = 1e-05


def rope_tables(position):
    halves = HEAD_SIZE // 2
    inverse = ROPE_BASE ** (-2.0 * jnp.arange(halves, dtype=jnp.float32) / HEAD_SIZE)
    angles = position.astype(jnp.float32)[:, None] * inverse[None, :]
    cosine = jnp.concatenate([jnp.cos(angles), jnp.cos(angles)], axis=1)
    sine_tab = jnp.concatenate([jnp.sin(angles), jnp.sin(angles)], axis=1)
    return (cosine, sine_tab)


def rotate(field, cosine, sine_tab):
    halves = HEAD_SIZE // 2
    turned = jnp.concatenate([-field[..., halves:], field[..., :halves]], axis=-1)
    return field * cosine[:, None, :] + turned * sine_tab[:, None, :]


def turn_matrix(cols):
    halves = HEAD_SIZE // 2
    c_in = jnp.arange(cols, dtype=jnp.int32)[:, None]
    c_out = jnp.arange(cols, dtype=jnp.int32)[None, :]
    local = c_out % HEAD_SIZE
    same_head = (c_in // HEAD_SIZE) == (c_out // HEAD_SIZE)
    low = same_head & (local < halves) & (c_in % HEAD_SIZE == local + halves)
    high = same_head & (local >= halves) & (c_in % HEAD_SIZE == local - halves)
    return jnp.where(low, -1.0, jnp.where(high, 1.0, 0.0)).astype(jnp.bfloat16)


def rotate_flat(field, cosine, sine_tab, turn):
    heads = field.shape[1] // HEAD_SIZE
    turned = jnp.dot(field, turn, preferred_element_type=jnp.float32)
    cos_all = jnp.tile(cosine, (1, heads))
    sin_all = jnp.tile(sine_tab, (1, heads))
    return (field.astype(jnp.float32) * cos_all + turned * sin_all).astype(jnp.bfloat16)


def turn_rows(field, cos_rows, sin_rows, turn):
    turned = jnp.dot(field, turn, preferred_element_type=jnp.float32)
    return (field.astype(jnp.float32) * cos_rows + turned * sin_rows).astype(jnp.bfloat16)


def head_select(cols, lanes):
    heads = cols // HEAD_SIZE
    head = jnp.arange(heads, dtype=jnp.int32)[:, None, None]
    col = jnp.arange(cols, dtype=jnp.int32)[None, :, None]
    lane = jnp.arange(lanes, dtype=jnp.int32)[None, None, :]
    return ((col == head * HEAD_SIZE + lane) & (lane < HEAD_SIZE)).astype(jnp.bfloat16)


def attend_kernel(
    q_ref, kn_ref, vn_ref, kc_ref, vc_ref, cos_ref, sin_ref, turn_ref, sel_ref, selt_ref,
    qrank_ref, cache_ok_ref, krank_ref, o_ref, keys_ref, values_ref,
):
    step = pl.program_id(0)
    block = q_ref.shape[0]
    heads = sel_ref.shape[0]

    @pl.when(step == 0)
    def _():
        rotated = turn_rows(kn_ref[...], cos_ref[...], sin_ref[...], turn_ref[...])
        fresh = vn_ref[...]
        for head in range(heads):
            keys_ref[head] = jnp.dot(
                rotated, sel_ref[head], preferred_element_type=jnp.float32
            ).astype(jnp.bfloat16)
            values_ref[head] = jnp.dot(
                fresh, sel_ref[head], preferred_element_type=jnp.float32
            ).astype(jnp.bfloat16)

    here = pl.ds(pl.multiple_of(step * block, block), block)
    query = turn_rows(q_ref[...], cos_ref[here, :], sin_ref[here, :], turn_ref[...])
    score_scale = 1.0 / math.sqrt(HEAD_SIZE)
    cache_ok = cache_ok_ref[...] > 0
    new_ok = krank_ref[...] <= qrank_ref[...]
    contract = (((1,), (1,)), ((), ()))
    total = jnp.zeros(o_ref.shape, jnp.float32)
    for head in range(heads):
        head_query = jnp.dot(query, sel_ref[head], preferred_element_type=jnp.float32).astype(
            jnp.bfloat16
        )
        score_c = lax.dot_general(
            head_query, kc_ref[head], contract, preferred_element_type=jnp.float32
        ) * score_scale
        score_n = lax.dot_general(
            head_query, keys_ref[head], contract, preferred_element_type=jnp.float32
        ) * score_scale
        score_c = jnp.where(cache_ok, score_c, -1e30)
        score_n = jnp.where(new_ok, score_n, -1e30)
        top = jnp.maximum(
            jnp.max(score_c, axis=1, keepdims=True), jnp.max(score_n, axis=1, keepdims=True)
        )
        weight_c = jnp.exp(score_c - top)
        weight_n = jnp.exp(score_n - top)
        whole = jnp.sum(weight_c, axis=1, keepdims=True) + jnp.sum(weight_n, axis=1, keepdims=True)
        prob_c = (weight_c / whole).astype(jnp.bfloat16)
        prob_n = (weight_n / whole).astype(jnp.bfloat16)
        head_out = jnp.dot(prob_c, vc_ref[head], preferred_element_type=jnp.float32) + jnp.dot(
            prob_n, values_ref[head], preferred_element_type=jnp.float32
        )
        total = total + jnp.dot(
            head_out.astype(jnp.bfloat16), selt_ref[head], preferred_element_type=jnp.float32
        )
    o_ref[...] = total.astype(o_ref.dtype)


def attend_slots(query, fresh_keys, fresh_values, cache_keys, cache_values, cos_all, sin_all, turn,
                 q_rank, cache_ok, k_rank, slot_cap):
    rows, cols = query.shape
    block = rows // slot_cap
    span = cache_keys.shape[0]
    heads = cols // HEAD_SIZE
    lanes = 128
    sel = head_select(cols, lanes)
    sel_t = sel.transpose(0, 2, 1)
    split = lambda x: jnp.pad(
        x.reshape(x.shape[0], heads, HEAD_SIZE), ((0, 0), (0, 0), (0, lanes - HEAD_SIZE))
    ).transpose(1, 0, 2)
    whole = lambda i: (0, 0)
    whole3 = lambda i: (0, 0, 0)
    return pl.pallas_call(
        attend_kernel,
        out_shape=jax.ShapeDtypeStruct((block, slot_cap * cols), jnp.bfloat16),
        grid=(slot_cap,),
        in_specs=[
            pl.BlockSpec((block, cols), lambda i: (i, 0)),
            pl.BlockSpec((rows, cols), whole),
            pl.BlockSpec((rows, cols), whole),
            pl.BlockSpec((heads, span, lanes), whole3),
            pl.BlockSpec((heads, span, lanes), whole3),
            pl.BlockSpec((rows, cols), whole),
            pl.BlockSpec((rows, cols), whole),
            pl.BlockSpec((cols, cols), whole),
            pl.BlockSpec((heads, cols, lanes), whole3),
            pl.BlockSpec((heads, lanes, cols), whole3),
            pl.BlockSpec((block, 1), lambda i: (i, 0)),
            pl.BlockSpec((1, span), whole),
            pl.BlockSpec((1, rows), whole),
        ],
        out_specs=pl.BlockSpec((block, cols), lambda i: (0, i)),
        scratch_shapes=[
            pltpu.VMEM((heads, rows, lanes), jnp.bfloat16),
            pltpu.VMEM((heads, rows, lanes), jnp.bfloat16),
        ],
        compiler_params=pltpu.CompilerParams(dimension_semantics=("arbitrary",)),
    )(query, fresh_keys, fresh_values, split(cache_keys), split(cache_values), cos_all, sin_all,
      turn, sel, sel_t, q_rank, cache_ok, k_rank)


def on_device(
    qkv_rows,
    row_request,
    request_owner,
    cached_len,
    page_table,
    kv_pages,
    residual,
    out_weight,
    norm_gain,
):
    row_count = qkv_rows.shape[0]
    parts = qkv_rows.shape[1]
    head_cols = qkv_rows.shape[2]
    heads_here = head_cols // HEAD_SIZE
    devices = lax.axis_size("req")
    slot_cap = SLOT
    buffer_len = devices * slot_cap
    device_ids = jnp.arange(devices, dtype=jnp.int32)
    row_ids = jnp.arange(row_count, dtype=jnp.int32)

    weight_cols = lax.all_to_all(out_weight, "tp", split_axis=1, concat_axis=0, tiled=True)
    owner_dev = request_owner[row_request]
    same_owner = owner_dev[:, None] == owner_dev[None, :]
    slot_in = jnp.sum((same_owner & (row_ids[None, :] < row_ids[:, None])).astype(jnp.int32), axis=1)
    sends_to = owner_dev[:, None] == device_ids[None, :]
    counts = jnp.sum(sends_to.astype(jnp.int32), axis=0)

    pick = (
        sends_to[None, :, :]
        & (slot_in[None, :, None] == jnp.arange(slot_cap, dtype=jnp.int32)[:, None, None])
    ).astype(jnp.bfloat16)
    slots = jnp.einsum(
        "jid,ipc->dpjc", pick, qkv_rows, preferred_element_type=jnp.float32
    ).astype(jnp.bfloat16)
    count_row = jnp.broadcast_to(counts.astype(jnp.bfloat16)[:, None, None], (devices, 1, head_cols))
    outgoing = jnp.concatenate(
        [slots.reshape(devices, slot_cap * parts, head_cols), count_row], axis=1
    )
    arrived = lax.all_to_all(outgoing, "req", split_axis=0, concat_axis=0, tiled=True)
    planes = arrived.transpose(1, 0, 2)
    arrived_counts = planes[slot_cap * parts, :, 0].astype(jnp.int32)

    length = cached_len[0]
    pool_pages = kv_pages[page_table[0]]
    cache_span = pool_pages.shape[0] * pool_pages.shape[2]
    cache_keys = pool_pages[:, 0].reshape(cache_span, head_cols)
    cache_values = pool_pages[:, 1].reshape(cache_span, head_cols)
    slot_of = jnp.arange(slot_cap, dtype=jnp.int32)[:, None]
    before = jnp.cumsum(arrived_counts) - arrived_counts
    live_slot = (slot_of < arrived_counts[None, :]).reshape(buffer_len)
    new_rank = (before[None, :] + slot_of).reshape(buffer_len)
    cosine, sine_tab = rope_tables(length + new_rank)
    cos_all = jnp.tile(cosine, (1, heads_here))
    sin_all = jnp.tile(sine_tab, (1, heads_here))
    cache_ok = (jnp.arange(cache_span, dtype=jnp.int32) < length).astype(jnp.int32)[None, :]
    k_rank = jnp.where(live_slot, new_rank, jnp.int32(2**30))[None, :]
    q_rank = new_rank[:, None]
    part_rows = [
        planes[p * slot_cap : (p + 1) * slot_cap].reshape(buffer_len, head_cols)
        for p in range(parts)
    ]
    result = attend_slots(
        part_rows[0], part_rows[1], part_rows[2], cache_keys, cache_values, cos_all, sin_all,
        turn_matrix(head_cols), q_rank, cache_ok, k_rank, slot_cap,
    )
    returned = lax.all_to_all(
        result.reshape(devices, slot_cap * parts, head_cols // parts),
        "req",
        split_axis=0,
        concat_axis=0,
        tiled=True,
    )
    target = owner_dev * slot_cap + slot_in
    attn_rows = returned.reshape(buffer_len, head_cols)[target]
    attn_all = lax.all_gather(attn_rows, "tp", axis=1, tiled=True)
    mixed_cols = jnp.dot(attn_all, weight_cols, preferred_element_type=jnp.float32)
    hidden = residual.astype(jnp.float32) + mixed_cols
    square_sum = lax.psum(jnp.sum(hidden * hidden, axis=1), "tp")
    inv_rms = lax.rsqrt(square_sum / D + EPS)
    normed = hidden * inv_rms[:, None] * norm_gain.astype(jnp.float32)[None, :]
    return (hidden.astype(jnp.bfloat16), normed.astype(jnp.bfloat16))


def solution(mesh):
    return jax.shard_map(
        on_device,
        mesh=mesh,
        in_specs=(
            P("req", None, "tp"),
            P("req"),
            P(),
            P("req"),
            P("req", None),
            P("req", None, None, "tp"),
            P("req", "tp"),
            P("tp", None),
            P("tp"),
        ),
        out_specs=(P("req", "tp"), P("req", "tp")),
        check_vma=False,
    )
```

```python
import math

import jax
import jax.numpy as jnp
from jax import lax
from jax.experimental import pallas as pl
from jax.experimental.pallas import tpu as pltpu
from jax.sharding import PartitionSpec as P

D = 3072
HEAD_SIZE = 96
SLOT = 5

ROPE_BASE = 10000.0
EPS = 1e-05


def rope_tables(position):
    halves = HEAD_SIZE // 2
    inverse = ROPE_BASE ** (-2.0 * jnp.arange(halves, dtype=jnp.float32) / HEAD_SIZE)
    angles = position.astype(jnp.float32)[:, None] * inverse[None, :]
    cosine = jnp.concatenate([jnp.cos(angles), jnp.cos(angles)], axis=1)
    sine_tab = jnp.concatenate([jnp.sin(angles), jnp.sin(angles)], axis=1)
    return (cosine, sine_tab)


def rotate(field, cosine, sine_tab):
    halves = HEAD_SIZE // 2
    turned = jnp.concatenate([-field[..., halves:], field[..., :halves]], axis=-1)
    return field * cosine[:, None, :] + turned * sine_tab[:, None, :]


def turn_matrix(cols):
    halves = HEAD_SIZE // 2
    c_in = jnp.arange(cols, dtype=jnp.int32)[:, None]
    c_out = jnp.arange(cols, dtype=jnp.int32)[None, :]
    local = c_out % HEAD_SIZE
    same_head = (c_in // HEAD_SIZE) == (c_out // HEAD_SIZE)
    low = same_head & (local < halves) & (c_in % HEAD_SIZE == local + halves)
    high = same_head & (local >= halves) & (c_in % HEAD_SIZE == local - halves)
    return jnp.where(low, -1.0, jnp.where(high, 1.0, 0.0)).astype(jnp.bfloat16)


def rotate_flat(field, cosine, sine_tab, turn):
    heads = field.shape[1] // HEAD_SIZE
    turned = jnp.dot(field, turn, preferred_element_type=jnp.float32)
    cos_all = jnp.tile(cosine, (1, heads))
    sin_all = jnp.tile(sine_tab, (1, heads))
    return (field.astype(jnp.float32) * cos_all + turned * sin_all).astype(jnp.bfloat16)


def turn_rows(field, cos_rows, sin_rows, turn):
    turned = jnp.dot(field, turn, preferred_element_type=jnp.float32)
    return (field.astype(jnp.float32) * cos_rows + turned * sin_rows).astype(jnp.bfloat16)


def head_select(cols, lanes):
    heads = cols // HEAD_SIZE
    head = jnp.arange(heads, dtype=jnp.int32)[:, None, None]
    col = jnp.arange(cols, dtype=jnp.int32)[None, :, None]
    lane = jnp.arange(lanes, dtype=jnp.int32)[None, None, :]
    return ((col == head * HEAD_SIZE + lane) & (lane < HEAD_SIZE)).astype(jnp.bfloat16)


def attend_kernel(
    q_ref, kn_ref, vn_ref, kc_ref, vc_ref, cos_ref, sin_ref, turn_ref, sel_ref, selt_ref,
    qrank_ref, cache_ok_ref, krank_ref, o_ref, keys_ref, values_ref,
):
    step = pl.program_id(0)
    block = q_ref.shape[0]
    heads = sel_ref.shape[0]

    @pl.when(step == 0)
    def _():
        rotated = turn_rows(kn_ref[...], cos_ref[...], sin_ref[...], turn_ref[...])
        fresh = vn_ref[...]
        for head in range(heads):
            keys_ref[head] = jnp.dot(
                rotated, sel_ref[head], preferred_element_type=jnp.float32
            ).astype(jnp.bfloat16)
            values_ref[head] = jnp.dot(
                fresh, sel_ref[head], preferred_element_type=jnp.float32
            ).astype(jnp.bfloat16)

    here = pl.ds(pl.multiple_of(step * block, block), block)
    query = turn_rows(q_ref[...], cos_ref[here, :], sin_ref[here, :], turn_ref[...])
    score_scale = 1.0 / math.sqrt(HEAD_SIZE)
    cache_ok = cache_ok_ref[...] > 0
    new_ok = krank_ref[...] <= qrank_ref[...]
    contract = (((1,), (1,)), ((), ()))
    total = jnp.zeros(o_ref.shape, jnp.float32)
    for head in range(heads):
        head_query = jnp.dot(query, sel_ref[head], preferred_element_type=jnp.float32).astype(
            jnp.bfloat16
        )
        score_c = lax.dot_general(
            head_query, kc_ref[head], contract, preferred_element_type=jnp.float32
        ) * score_scale
        score_n = lax.dot_general(
            head_query, keys_ref[head], contract, preferred_element_type=jnp.float32
        ) * score_scale
        score_c = jnp.where(cache_ok, score_c, -1e30)
        score_n = jnp.where(new_ok, score_n, -1e30)
        top = jnp.maximum(
            jnp.max(score_c, axis=1, keepdims=True), jnp.max(score_n, axis=1, keepdims=True)
        )
        weight_c = jnp.exp(score_c - top)
        weight_n = jnp.exp(score_n - top)
        whole = jnp.sum(weight_c, axis=1, keepdims=True) + jnp.sum(weight_n, axis=1, keepdims=True)
        prob_c = (weight_c / whole).astype(jnp.bfloat16)
        prob_n = (weight_n / whole).astype(jnp.bfloat16)
        head_out = jnp.dot(prob_c, vc_ref[head], preferred_element_type=jnp.float32) + jnp.dot(
            prob_n, values_ref[head], preferred_element_type=jnp.float32
        )
        total = total + jnp.dot(
            head_out.astype(jnp.bfloat16), selt_ref[head], preferred_element_type=jnp.float32
        )
    o_ref[...] = total.astype(o_ref.dtype)


def attend_slots(query, fresh_keys, fresh_values, cache_keys, cache_values, cos_all, sin_all, turn,
                 q_rank, cache_ok, k_rank, slot_cap):
    rows, cols = query.shape
    block = rows // slot_cap
    span = cache_keys.shape[0]
    heads = cols // HEAD_SIZE
    lanes = 128
    sel = head_select(cols, lanes)
    sel_t = sel.transpose(0, 2, 1)
    split = lambda x: jnp.pad(
        x.reshape(x.shape[0], heads, HEAD_SIZE), ((0, 0), (0, 0), (0, lanes - HEAD_SIZE))
    ).transpose(1, 0, 2)
    whole = lambda i: (0, 0)
    whole3 = lambda i: (0, 0, 0)
    return pl.pallas_call(
        attend_kernel,
        out_shape=jax.ShapeDtypeStruct((block, slot_cap * cols), jnp.bfloat16),
        grid=(slot_cap,),
        in_specs=[
            pl.BlockSpec((block, cols), lambda i: (i, 0)),
            pl.BlockSpec((rows, cols), whole),
            pl.BlockSpec((rows, cols), whole),
            pl.BlockSpec((heads, span, lanes), whole3),
            pl.BlockSpec((heads, span, lanes), whole3),
            pl.BlockSpec((rows, cols), whole),
            pl.BlockSpec((rows, cols), whole),
            pl.BlockSpec((cols, cols), whole),
            pl.BlockSpec((heads, cols, lanes), whole3),
            pl.BlockSpec((heads, lanes, cols), whole3),
            pl.BlockSpec((block, 1), lambda i: (i, 0)),
            pl.BlockSpec((1, span), whole),
            pl.BlockSpec((1, rows), whole),
        ],
        out_specs=pl.BlockSpec((block, cols), lambda i: (0, i)),
        scratch_shapes=[
            pltpu.VMEM((heads, rows, lanes), jnp.bfloat16),
            pltpu.VMEM((heads, rows, lanes), jnp.bfloat16),
        ],
        compiler_params=pltpu.CompilerParams(dimension_semantics=("arbitrary",)),
    )(query, fresh_keys, fresh_values, split(cache_keys), split(cache_values), cos_all, sin_all,
      turn, sel, sel_t, q_rank, cache_ok, k_rank)


def on_device(
    qkv_rows,
    row_request,
    request_owner,
    cached_len,
    page_table,
    kv_pages,
    residual,
    out_weight,
    norm_gain,
):
    row_count = qkv_rows.shape[0]
    parts = qkv_rows.shape[1]
    head_cols = qkv_rows.shape[2]
    heads_here = head_cols // HEAD_SIZE
    devices = lax.axis_size("req")
    slot_cap = SLOT
    buffer_len = devices * slot_cap
    device_ids = jnp.arange(devices, dtype=jnp.int32)
    row_ids = jnp.arange(row_count, dtype=jnp.int32)

    weight_cols = lax.all_to_all(out_weight, "tp", split_axis=1, concat_axis=0, tiled=True)
    owner_dev = request_owner[row_request]
    same_owner = owner_dev[:, None] == owner_dev[None, :]
    slot_in = jnp.sum((same_owner & (row_ids[None, :] < row_ids[:, None])).astype(jnp.int32), axis=1)
    sends_to = owner_dev[:, None] == device_ids[None, :]
    counts = jnp.sum(sends_to.astype(jnp.int32), axis=0)

    pick = (
        sends_to[None, :, :]
        & (slot_in[None, :, None] == jnp.arange(slot_cap, dtype=jnp.int32)[:, None, None])
    ).astype(jnp.bfloat16)
    slots = jnp.einsum(
        "jid,ipc->dpjc", pick, qkv_rows, preferred_element_type=jnp.float32
    ).astype(jnp.bfloat16)
    count_row = jnp.broadcast_to(counts.astype(jnp.bfloat16)[:, None, None], (devices, 1, head_cols))
    outgoing = jnp.concatenate(
        [slots.reshape(devices, slot_cap * parts, head_cols), count_row], axis=1
    )
    arrived = lax.all_to_all(outgoing, "req", split_axis=0, concat_axis=0, tiled=True)
    planes = arrived.transpose(1, 0, 2)
    arrived_counts = planes[slot_cap * parts, :, 0].astype(jnp.int32)

    length = cached_len[0]
    pool_pages = kv_pages[page_table[0]]
    cache_span = pool_pages.shape[0] * pool_pages.shape[2]
    cache_keys = pool_pages[:, 0].reshape(cache_span, head_cols)
    cache_values = pool_pages[:, 1].reshape(cache_span, head_cols)
    slot_of = jnp.arange(slot_cap, dtype=jnp.int32)[:, None]
    before = jnp.cumsum(arrived_counts) - arrived_counts
    live_slot = (slot_of < arrived_counts[None, :]).reshape(buffer_len)
    new_rank = (before[None, :] + slot_of).reshape(buffer_len)
    cosine, sine_tab = rope_tables(length + new_rank)
    cos_all = jnp.tile(cosine, (1, heads_here))
    sin_all = jnp.tile(sine_tab, (1, heads_here))
    cache_ok = (jnp.arange(cache_span, dtype=jnp.int32) < length).astype(jnp.int32)[None, :]
    k_rank = jnp.where(live_slot, new_rank, jnp.int32(2**30))[None, :]
    q_rank = new_rank[:, None]
    part_rows = [
        planes[p * slot_cap : (p + 1) * slot_cap].reshape(buffer_len, head_cols)
        for p in range(parts)
    ]
    result = attend_slots(
        part_rows[0], part_rows[1], part_rows[2], cache_keys, cache_values, cos_all, sin_all,
        turn_matrix(head_cols), q_rank, cache_ok, k_rank, slot_cap,
    )
    returned = lax.all_to_all(
        result.reshape(devices, slot_cap * parts, head_cols // parts),
        "req",
        split_axis=0,
        concat_axis=0,
        tiled=True,
    )
    target = owner_dev * slot_cap + slot_in
    attn_rows = returned.reshape(buffer_len, head_cols)[target]
    attn_all = lax.all_gather(attn_rows, "tp", axis=1, tiled=True)
    mixed_cols = jnp.dot(attn_all, weight_cols, preferred_element_type=jnp.float32)
    hidden = residual.astype(jnp.float32) + mixed_cols
    square_part = jnp.sum(hidden * hidden, axis=1)
    tp_size = lax.axis_size("tp")
    square_sum = jnp.sum(
        lax.all_to_all(
            jnp.broadcast_to(square_part[None], (tp_size,) + square_part.shape), "tp", 0, 0, tiled=True
        ),
        axis=0,
    )
    inv_rms = lax.rsqrt(square_sum / D + EPS)
    normed = hidden * inv_rms[:, None] * norm_gain.astype(jnp.float32)[None, :]
    return (hidden.astype(jnp.bfloat16), normed.astype(jnp.bfloat16))


def solution(mesh):
    return jax.shard_map(
        on_device,
        mesh=mesh,
        in_specs=(
            P("req", None, "tp"),
            P("req"),
            P(),
            P("req"),
            P("req", None),
            P("req", None, None, "tp"),
            P("req", "tp"),
            P("tp", None),
            P("tp"),
        ),
        out_specs=(P("req", "tp"), P("req", "tp")),
        check_vma=False,
    )
```

```python
import math

import jax
import jax.numpy as jnp
from jax import lax
from jax.experimental import pallas as pl
from jax.experimental.pallas import tpu as pltpu
from jax.sharding import PartitionSpec as P

D = 3072
HEAD_SIZE = 96
SLOT = 5

ROPE_BASE = 10000.0
EPS = 1e-05


def rope_tables(position):
    halves = HEAD_SIZE // 2
    inverse = ROPE_BASE ** (-2.0 * jnp.arange(halves, dtype=jnp.float32) / HEAD_SIZE)
    angles = position.astype(jnp.float32)[:, None] * inverse[None, :]
    cosine = jnp.concatenate([jnp.cos(angles), jnp.cos(angles)], axis=1)
    sine_tab = jnp.concatenate([jnp.sin(angles), jnp.sin(angles)], axis=1)
    return (cosine, sine_tab)


def rotate(field, cosine, sine_tab):
    halves = HEAD_SIZE // 2
    turned = jnp.concatenate([-field[..., halves:], field[..., :halves]], axis=-1)
    return field * cosine[:, None, :] + turned * sine_tab[:, None, :]


def turn_matrix(cols):
    halves = HEAD_SIZE // 2
    c_in = jnp.arange(cols, dtype=jnp.int32)[:, None]
    c_out = jnp.arange(cols, dtype=jnp.int32)[None, :]
    local = c_out % HEAD_SIZE
    same_head = (c_in // HEAD_SIZE) == (c_out // HEAD_SIZE)
    low = same_head & (local < halves) & (c_in % HEAD_SIZE == local + halves)
    high = same_head & (local >= halves) & (c_in % HEAD_SIZE == local - halves)
    return jnp.where(low, -1.0, jnp.where(high, 1.0, 0.0)).astype(jnp.bfloat16)


def rotate_flat(field, cosine, sine_tab, turn):
    heads = field.shape[1] // HEAD_SIZE
    turned = jnp.dot(field, turn, preferred_element_type=jnp.float32)
    cos_all = jnp.tile(cosine, (1, heads))
    sin_all = jnp.tile(sine_tab, (1, heads))
    return (field.astype(jnp.float32) * cos_all + turned * sin_all).astype(jnp.bfloat16)


def turn_rows(field, cos_rows, sin_rows, turn):
    turned = jnp.dot(field, turn, preferred_element_type=jnp.float32)
    return (field.astype(jnp.float32) * cos_rows + turned * sin_rows).astype(jnp.bfloat16)


def head_select(cols, lanes):
    heads = cols // HEAD_SIZE
    head = jnp.arange(heads, dtype=jnp.int32)[:, None, None]
    col = jnp.arange(cols, dtype=jnp.int32)[None, :, None]
    lane = jnp.arange(lanes, dtype=jnp.int32)[None, None, :]
    return ((col == head * HEAD_SIZE + lane) & (lane < HEAD_SIZE)).astype(jnp.bfloat16)


def attend_kernel(
    q_ref, kn_ref, vn_ref, kc_ref, vc_ref, cos_ref, sin_ref, turn_ref, sel_ref, selt_ref,
    qrank_ref, cache_ok_ref, krank_ref, o_ref, keys_ref, values_ref,
):
    step = pl.program_id(0)
    block = q_ref.shape[0]
    heads = sel_ref.shape[0]

    @pl.when(step == 0)
    def _():
        rotated = turn_rows(kn_ref[...], cos_ref[...], sin_ref[...], turn_ref[...])
        fresh = vn_ref[...]
        for head in range(heads):
            keys_ref[head] = jnp.dot(
                rotated, sel_ref[head], preferred_element_type=jnp.float32
            ).astype(jnp.bfloat16)
            values_ref[head] = jnp.dot(
                fresh, sel_ref[head], preferred_element_type=jnp.float32
            ).astype(jnp.bfloat16)

    here = pl.ds(pl.multiple_of(step * block, block), block)
    query = turn_rows(q_ref[...], cos_ref[here, :], sin_ref[here, :], turn_ref[...])
    score_scale = 1.0 / math.sqrt(HEAD_SIZE)
    cache_ok = cache_ok_ref[...] > 0
    new_ok = krank_ref[...] <= qrank_ref[...]
    contract = (((1,), (1,)), ((), ()))
    total = jnp.zeros(o_ref.shape, jnp.float32)
    for head in range(heads):
        head_query = jnp.dot(query, sel_ref[head], preferred_element_type=jnp.float32).astype(
            jnp.bfloat16
        )
        score_c = lax.dot_general(
            head_query, kc_ref[head], contract, preferred_element_type=jnp.float32
        ) * score_scale
        score_n = lax.dot_general(
            head_query, keys_ref[head], contract, preferred_element_type=jnp.float32
        ) * score_scale
        score_c = jnp.where(cache_ok, score_c, -1e30)
        score_n = jnp.where(new_ok, score_n, -1e30)
        top = jnp.maximum(
            jnp.max(score_c, axis=1, keepdims=True), jnp.max(score_n, axis=1, keepdims=True)
        )
        weight_c = jnp.exp(score_c - top)
        weight_n = jnp.exp(score_n - top)
        whole = jnp.sum(weight_c, axis=1, keepdims=True) + jnp.sum(weight_n, axis=1, keepdims=True)
        prob_c = (weight_c / whole).astype(jnp.bfloat16)
        prob_n = (weight_n / whole).astype(jnp.bfloat16)
        head_out = jnp.dot(prob_c, vc_ref[head], preferred_element_type=jnp.float32) + jnp.dot(
            prob_n, values_ref[head], preferred_element_type=jnp.float32
        )
        total = total + jnp.dot(
            head_out.astype(jnp.bfloat16), selt_ref[head], preferred_element_type=jnp.float32
        )
    o_ref[...] = total.astype(o_ref.dtype)


def attend_slots(query, fresh_keys, fresh_values, cache_keys, cache_values, cos_all, sin_all, turn,
                 q_rank, cache_ok, k_rank, slot_cap):
    rows, cols = query.shape
    block = rows // slot_cap
    span = cache_keys.shape[0]
    heads = cols // HEAD_SIZE
    lanes = 128
    sel = head_select(cols, lanes)
    sel_t = sel.transpose(0, 2, 1)
    split = lambda x: jnp.pad(
        x.reshape(x.shape[0], heads, HEAD_SIZE), ((0, 0), (0, 0), (0, lanes - HEAD_SIZE))
    ).transpose(1, 0, 2)
    whole = lambda i: (0, 0)
    whole3 = lambda i: (0, 0, 0)
    return pl.pallas_call(
        attend_kernel,
        out_shape=jax.ShapeDtypeStruct((block, slot_cap * cols), jnp.bfloat16),
        grid=(slot_cap,),
        in_specs=[
            pl.BlockSpec((block, cols), lambda i: (i, 0)),
            pl.BlockSpec((rows, cols), whole),
            pl.BlockSpec((rows, cols), whole),
            pl.BlockSpec((heads, span, lanes), whole3),
            pl.BlockSpec((heads, span, lanes), whole3),
            pl.BlockSpec((rows, cols), whole),
            pl.BlockSpec((rows, cols), whole),
            pl.BlockSpec((cols, cols), whole),
            pl.BlockSpec((heads, cols, lanes), whole3),
            pl.BlockSpec((heads, lanes, cols), whole3),
            pl.BlockSpec((block, 1), lambda i: (i, 0)),
            pl.BlockSpec((1, span), whole),
            pl.BlockSpec((1, rows), whole),
        ],
        out_specs=pl.BlockSpec((block, cols), lambda i: (0, i)),
        scratch_shapes=[
            pltpu.VMEM((heads, rows, lanes), jnp.bfloat16),
            pltpu.VMEM((heads, rows, lanes), jnp.bfloat16),
        ],
        compiler_params=pltpu.CompilerParams(dimension_semantics=("arbitrary",)),
    )(query, fresh_keys, fresh_values, split(cache_keys), split(cache_values), cos_all, sin_all,
      turn, sel, sel_t, q_rank, cache_ok, k_rank)


def on_device(
    qkv_rows,
    row_request,
    request_owner,
    cached_len,
    page_table,
    kv_pages,
    residual,
    out_weight,
    norm_gain,
):
    row_count = qkv_rows.shape[0]
    parts = qkv_rows.shape[1]
    head_cols = qkv_rows.shape[2]
    heads_here = head_cols // HEAD_SIZE
    devices = lax.axis_size("req")
    slot_cap = SLOT
    buffer_len = devices * slot_cap
    device_ids = jnp.arange(devices, dtype=jnp.int32)
    row_ids = jnp.arange(row_count, dtype=jnp.int32)

    weight_cols = lax.all_to_all(out_weight, "tp", split_axis=1, concat_axis=0, tiled=True)
    owner_dev = request_owner[row_request]
    same_owner = owner_dev[:, None] == owner_dev[None, :]
    slot_in = jnp.sum((same_owner & (row_ids[None, :] < row_ids[:, None])).astype(jnp.int32), axis=1)
    sends_to = owner_dev[:, None] == device_ids[None, :]
    counts = jnp.sum(sends_to.astype(jnp.int32), axis=0)

    pick = (
        sends_to[None, :, :]
        & (slot_in[None, :, None] == jnp.arange(slot_cap, dtype=jnp.int32)[:, None, None])
    ).astype(jnp.bfloat16)
    slots = jnp.einsum(
        "jid,ipc->dpjc", pick, qkv_rows, preferred_element_type=jnp.float32
    ).astype(jnp.bfloat16)
    count_row = jnp.broadcast_to(counts.astype(jnp.bfloat16)[:, None, None], (devices, 1, head_cols))
    outgoing = jnp.concatenate(
        [slots.reshape(devices, slot_cap * parts, head_cols), count_row], axis=1
    )
    arrived = lax.all_to_all(outgoing, "req", split_axis=0, concat_axis=0, tiled=True)
    planes = arrived.transpose(1, 0, 2)
    arrived_counts = planes[slot_cap * parts, :, 0].astype(jnp.int32)

    length = cached_len[0]
    pool_pages = kv_pages[page_table[0]]
    cache_span = pool_pages.shape[0] * pool_pages.shape[2]
    cache_keys = pool_pages[:, 0].reshape(cache_span, head_cols)
    cache_values = pool_pages[:, 1].reshape(cache_span, head_cols)
    slot_of = jnp.arange(slot_cap, dtype=jnp.int32)[:, None]
    before = jnp.cumsum(arrived_counts) - arrived_counts
    live_slot = (slot_of < arrived_counts[None, :]).reshape(buffer_len)
    new_rank = (before[None, :] + slot_of).reshape(buffer_len)
    cosine, sine_tab = rope_tables(length + jnp.arange(buffer_len, dtype=jnp.int32))
    cos_all = jnp.take(jnp.tile(cosine, (1, heads_here)), new_rank, axis=0, mode="clip")
    sin_all = jnp.take(jnp.tile(sine_tab, (1, heads_here)), new_rank, axis=0, mode="clip")
    cache_ok = (jnp.arange(cache_span, dtype=jnp.int32) < length).astype(jnp.int32)[None, :]
    k_rank = jnp.where(live_slot, new_rank, jnp.int32(2**30))[None, :]
    q_rank = new_rank[:, None]
    part_rows = [
        planes[p * slot_cap : (p + 1) * slot_cap].reshape(buffer_len, head_cols)
        for p in range(parts)
    ]
    result = attend_slots(
        part_rows[0], part_rows[1], part_rows[2], cache_keys, cache_values, cos_all, sin_all,
        turn_matrix(head_cols), q_rank, cache_ok, k_rank, slot_cap,
    )
    returned = lax.all_to_all(
        result.reshape(devices, slot_cap * parts, head_cols // parts),
        "req",
        split_axis=0,
        concat_axis=0,
        tiled=True,
    )
    target = owner_dev * slot_cap + slot_in
    attn_rows = returned.reshape(buffer_len, head_cols)[target]
    attn_all = lax.all_gather(attn_rows, "tp", axis=1, tiled=True)
    mixed_cols = jnp.dot(attn_all, weight_cols, preferred_element_type=jnp.float32)
    hidden = residual.astype(jnp.float32) + mixed_cols
    square_part = jnp.sum(hidden * hidden, axis=1)
    tp_size = lax.axis_size("tp")
    square_sum = jnp.sum(
        lax.all_to_all(
            jnp.broadcast_to(square_part[None], (tp_size,) + square_part.shape), "tp", 0, 0, tiled=True
        ),
        axis=0,
    )
    inv_rms = lax.rsqrt(square_sum / D + EPS)
    normed = hidden * inv_rms[:, None] * norm_gain.astype(jnp.float32)[None, :]
    return (hidden.astype(jnp.bfloat16), normed.astype(jnp.bfloat16))


def solution(mesh):
    return jax.shard_map(
        on_device,
        mesh=mesh,
        in_specs=(
            P("req", None, "tp"),
            P("req"),
            P(),
            P("req"),
            P("req", None),
            P("req", None, None, "tp"),
            P("req", "tp"),
            P("tp", None),
            P("tp"),
        ),
        out_specs=(P("req", "tp"), P("req", "tp")),
        check_vma=False,
    )
```

```python
import math

import jax
import jax.numpy as jnp
from jax import lax
from jax.experimental import pallas as pl
from jax.experimental.pallas import tpu as pltpu
from jax.sharding import PartitionSpec as P

D = 3072
HEAD_SIZE = 96
SLOT = 5

ROPE_BASE = 10000.0
EPS = 1e-05


def rope_tables(position):
    halves = HEAD_SIZE // 2
    inverse = ROPE_BASE ** (-2.0 * jnp.arange(halves, dtype=jnp.float32) / HEAD_SIZE)
    angles = position.astype(jnp.float32)[:, None] * inverse[None, :]
    cosine = jnp.concatenate([jnp.cos(angles), jnp.cos(angles)], axis=1)
    sine_tab = jnp.concatenate([jnp.sin(angles), jnp.sin(angles)], axis=1)
    return (cosine, sine_tab)


def rotate(field, cosine, sine_tab):
    halves = HEAD_SIZE // 2
    turned = jnp.concatenate([-field[..., halves:], field[..., :halves]], axis=-1)
    return field * cosine[:, None, :] + turned * sine_tab[:, None, :]


def turn_matrix(cols):
    halves = HEAD_SIZE // 2
    c_in = jnp.arange(cols, dtype=jnp.int32)[:, None]
    c_out = jnp.arange(cols, dtype=jnp.int32)[None, :]
    local = c_out % HEAD_SIZE
    same_head = (c_in // HEAD_SIZE) == (c_out // HEAD_SIZE)
    low = same_head & (local < halves) & (c_in % HEAD_SIZE == local + halves)
    high = same_head & (local >= halves) & (c_in % HEAD_SIZE == local - halves)
    return jnp.where(low, -1.0, jnp.where(high, 1.0, 0.0)).astype(jnp.bfloat16)


def rotate_flat(field, cosine, sine_tab, turn):
    heads = field.shape[1] // HEAD_SIZE
    turned = jnp.dot(field, turn, preferred_element_type=jnp.float32)
    cos_all = jnp.tile(cosine, (1, heads))
    sin_all = jnp.tile(sine_tab, (1, heads))
    return (field.astype(jnp.float32) * cos_all + turned * sin_all).astype(jnp.bfloat16)


def turn_rows(field, cos_rows, sin_rows, turn):
    turned = jnp.dot(field, turn, preferred_element_type=jnp.float32)
    return (field.astype(jnp.float32) * cos_rows + turned * sin_rows).astype(jnp.bfloat16)


def head_select(cols, lanes):
    heads = cols // HEAD_SIZE
    head = jnp.arange(heads, dtype=jnp.int32)[:, None, None]
    col = jnp.arange(cols, dtype=jnp.int32)[None, :, None]
    lane = jnp.arange(lanes, dtype=jnp.int32)[None, None, :]
    return ((col == head * HEAD_SIZE + lane) & (lane < HEAD_SIZE)).astype(jnp.bfloat16)


def attend_kernel(
    q_ref, kn_ref, vn_ref, kc_ref, vc_ref, cos_ref, sin_ref, turn_ref, sel_ref, selt_ref,
    qrank_ref, cache_ok_ref, krank_ref, o_ref, keys_ref, values_ref,
):
    step = pl.program_id(0)
    block = q_ref.shape[0]
    heads = sel_ref.shape[0]

    @pl.when(step == 0)
    def _():
        rows = kn_ref.shape[0] * kn_ref.shape[1]
        rotated = turn_rows(
            kn_ref[...].reshape(rows, -1), cos_ref[...], sin_ref[...], turn_ref[...]
        )
        fresh = vn_ref[...].reshape(rows, -1)
        for head in range(heads):
            keys_ref[head] = jnp.dot(
                rotated, sel_ref[head], preferred_element_type=jnp.float32
            ).astype(jnp.bfloat16)
            values_ref[head] = jnp.dot(
                fresh, sel_ref[head], preferred_element_type=jnp.float32
            ).astype(jnp.bfloat16)

    here = pl.ds(pl.multiple_of(step * block, block), block)
    query = turn_rows(q_ref[...], cos_ref[here, :], sin_ref[here, :], turn_ref[...])
    score_scale = 1.0 / math.sqrt(HEAD_SIZE)
    cache_ok = cache_ok_ref[...] > 0
    new_ok = krank_ref[...] <= qrank_ref[...]
    contract = (((1,), (1,)), ((), ()))
    total = jnp.zeros(o_ref.shape, jnp.float32)
    for head in range(heads):
        head_query = jnp.dot(query, sel_ref[head], preferred_element_type=jnp.float32).astype(
            jnp.bfloat16
        )
        score_c = lax.dot_general(
            head_query, kc_ref[head], contract, preferred_element_type=jnp.float32
        ) * score_scale
        score_n = lax.dot_general(
            head_query, keys_ref[head], contract, preferred_element_type=jnp.float32
        ) * score_scale
        score_c = jnp.where(cache_ok, score_c, -1e30)
        score_n = jnp.where(new_ok, score_n, -1e30)
        top = jnp.maximum(
            jnp.max(score_c, axis=1, keepdims=True), jnp.max(score_n, axis=1, keepdims=True)
        )
        weight_c = jnp.exp(score_c - top)
        weight_n = jnp.exp(score_n - top)
        whole = jnp.sum(weight_c, axis=1, keepdims=True) + jnp.sum(weight_n, axis=1, keepdims=True)
        prob_c = (weight_c / whole).astype(jnp.bfloat16)
        prob_n = (weight_n / whole).astype(jnp.bfloat16)
        head_out = jnp.dot(prob_c, vc_ref[head], preferred_element_type=jnp.float32) + jnp.dot(
            prob_n, values_ref[head], preferred_element_type=jnp.float32
        )
        total = total + jnp.dot(
            head_out.astype(jnp.bfloat16), selt_ref[head], preferred_element_type=jnp.float32
        )
    o_ref[...] = total.astype(o_ref.dtype)


def attend_slots(planes, cache_keys, cache_values, cos_all, sin_all, turn,
                 q_rank, cache_ok, k_rank, slot_cap):
    _, block, cols = planes.shape
    rows = slot_cap * block
    span = cache_keys.shape[0]
    heads = cols // HEAD_SIZE
    lanes = 128
    sel = head_select(cols, lanes)
    sel_t = sel.transpose(0, 2, 1)
    split = lambda x: jnp.pad(
        x.reshape(x.shape[0], heads, HEAD_SIZE), ((0, 0), (0, 0), (0, lanes - HEAD_SIZE))
    ).transpose(1, 0, 2)
    whole = lambda i: (0, 0)
    whole3 = lambda i: (0, 0, 0)
    return pl.pallas_call(
        attend_kernel,
        out_shape=jax.ShapeDtypeStruct((block, slot_cap * cols), jnp.bfloat16),
        grid=(slot_cap,),
        in_specs=[
            pl.BlockSpec((None, block, cols), lambda i: (i, 0, 0)),
            pl.BlockSpec((slot_cap, block, cols), lambda i: (1, 0, 0)),
            pl.BlockSpec((slot_cap, block, cols), lambda i: (2, 0, 0)),
            pl.BlockSpec((heads, span, lanes), whole3),
            pl.BlockSpec((heads, span, lanes), whole3),
            pl.BlockSpec((rows, cols), whole),
            pl.BlockSpec((rows, cols), whole),
            pl.BlockSpec((cols, cols), whole),
            pl.BlockSpec((heads, cols, lanes), whole3),
            pl.BlockSpec((heads, lanes, cols), whole3),
            pl.BlockSpec((block, 1), lambda i: (i, 0)),
            pl.BlockSpec((1, span), whole),
            pl.BlockSpec((1, rows), whole),
        ],
        out_specs=pl.BlockSpec((block, cols), lambda i: (0, i)),
        scratch_shapes=[
            pltpu.VMEM((heads, rows, lanes), jnp.bfloat16),
            pltpu.VMEM((heads, rows, lanes), jnp.bfloat16),
        ],
        compiler_params=pltpu.CompilerParams(dimension_semantics=("arbitrary",)),
    )(planes, planes, planes, split(cache_keys), split(cache_values), cos_all, sin_all,
      turn, sel, sel_t, q_rank, cache_ok, k_rank)


def on_device(
    qkv_rows,
    row_request,
    request_owner,
    cached_len,
    page_table,
    kv_pages,
    residual,
    out_weight,
    norm_gain,
):
    row_count = qkv_rows.shape[0]
    parts = qkv_rows.shape[1]
    head_cols = qkv_rows.shape[2]
    heads_here = head_cols // HEAD_SIZE
    devices = lax.axis_size("req")
    slot_cap = SLOT
    buffer_len = devices * slot_cap
    device_ids = jnp.arange(devices, dtype=jnp.int32)
    row_ids = jnp.arange(row_count, dtype=jnp.int32)

    weight_cols = lax.all_to_all(out_weight, "tp", split_axis=1, concat_axis=0, tiled=True)
    owner_dev = request_owner[row_request]
    same_owner = owner_dev[:, None] == owner_dev[None, :]
    slot_in = jnp.sum((same_owner & (row_ids[None, :] < row_ids[:, None])).astype(jnp.int32), axis=1)
    sends_to = owner_dev[:, None] == device_ids[None, :]
    counts = jnp.sum(sends_to.astype(jnp.int32), axis=0)

    pick = (
        sends_to[None, :, :]
        & (slot_in[None, :, None] == jnp.arange(slot_cap, dtype=jnp.int32)[:, None, None])
    ).astype(jnp.bfloat16)
    slots = jnp.einsum(
        "jid,ipc->dpjc", pick, qkv_rows, preferred_element_type=jnp.float32
    ).astype(jnp.bfloat16)
    count_row = jnp.broadcast_to(counts.astype(jnp.bfloat16)[:, None, None], (devices, 1, head_cols))
    outgoing = jnp.concatenate(
        [slots.reshape(devices, slot_cap * parts, head_cols), count_row], axis=1
    )
    arrived = lax.all_to_all(outgoing, "req", split_axis=0, concat_axis=0, tiled=True)
    planes = arrived.transpose(1, 0, 2)
    arrived_counts = planes[slot_cap * parts, :, 0].astype(jnp.int32)

    length = cached_len[0]
    pool_pages = kv_pages[page_table[0]]
    cache_span = pool_pages.shape[0] * pool_pages.shape[2]
    cache_keys = pool_pages[:, 0].reshape(cache_span, head_cols)
    cache_values = pool_pages[:, 1].reshape(cache_span, head_cols)
    slot_of = jnp.arange(slot_cap, dtype=jnp.int32)[:, None]
    before = jnp.cumsum(arrived_counts) - arrived_counts
    live_slot = (slot_of < arrived_counts[None, :]).reshape(buffer_len)
    new_rank = (before[None, :] + slot_of).reshape(buffer_len)
    cosine, sine_tab = rope_tables(length + new_rank)
    cos_all = jnp.tile(cosine, (1, heads_here))
    sin_all = jnp.tile(sine_tab, (1, heads_here))
    cache_ok = (jnp.arange(cache_span, dtype=jnp.int32) < length).astype(jnp.int32)[None, :]
    k_rank = jnp.where(live_slot, new_rank, jnp.int32(2**30))[None, :]
    q_rank = new_rank[:, None]
    result = attend_slots(
        planes, cache_keys, cache_values, cos_all, sin_all,
        turn_matrix(head_cols), q_rank, cache_ok, k_rank, slot_cap,
    )
    returned = lax.all_to_all(
        result.reshape(devices, slot_cap * parts, head_cols // parts),
        "req",
        split_axis=0,
        concat_axis=0,
        tiled=True,
    )
    target = owner_dev * slot_cap + slot_in
    attn_rows = returned.reshape(buffer_len, head_cols)[target]
    attn_all = lax.all_gather(attn_rows, "tp", axis=1, tiled=True)
    mixed_cols = jnp.dot(attn_all, weight_cols, preferred_element_type=jnp.float32)
    hidden = residual.astype(jnp.float32) + mixed_cols
    square_part = jnp.sum(hidden * hidden, axis=1)
    tp_size = lax.axis_size("tp")
    square_sum = jnp.sum(
        lax.all_to_all(
            jnp.broadcast_to(square_part[None], (tp_size,) + square_part.shape), "tp", 0, 0, tiled=True
        ),
        axis=0,
    )
    inv_rms = lax.rsqrt(square_sum / D + EPS)
    normed = hidden * inv_rms[:, None] * norm_gain.astype(jnp.float32)[None, :]
    return (hidden.astype(jnp.bfloat16), normed.astype(jnp.bfloat16))


def solution(mesh):
    return jax.shard_map(
        on_device,
        mesh=mesh,
        in_specs=(
            P("req", None, "tp"),
            P("req"),
            P(),
            P("req"),
            P("req", None),
            P("req", None, None, "tp"),
            P("req", "tp"),
            P("tp", None),
            P("tp"),
        ),
        out_specs=(P("req", "tp"), P("req", "tp")),
        check_vma=False,
    )
```

```python
import math

import jax
import jax.numpy as jnp
from jax import lax
from jax.experimental import pallas as pl
from jax.experimental.pallas import tpu as pltpu
from jax.sharding import PartitionSpec as P

D = 3072
HEAD_SIZE = 96
SLOT = 5

ROPE_BASE = 10000.0
EPS = 1e-05


def rope_tables(position):
    halves = HEAD_SIZE // 2
    inverse = ROPE_BASE ** (-2.0 * jnp.arange(halves, dtype=jnp.float32) / HEAD_SIZE)
    angles = position.astype(jnp.float32)[:, None] * inverse[None, :]
    cosine = jnp.concatenate([jnp.cos(angles), jnp.cos(angles)], axis=1)
    sine_tab = jnp.concatenate([jnp.sin(angles), jnp.sin(angles)], axis=1)
    return (cosine, sine_tab)


def rotate(field, cosine, sine_tab):
    halves = HEAD_SIZE // 2
    turned = jnp.concatenate([-field[..., halves:], field[..., :halves]], axis=-1)
    return field * cosine[:, None, :] + turned * sine_tab[:, None, :]


def turn_matrix(cols):
    halves = HEAD_SIZE // 2
    c_in = jnp.arange(cols, dtype=jnp.int32)[:, None]
    c_out = jnp.arange(cols, dtype=jnp.int32)[None, :]
    local = c_out % HEAD_SIZE
    same_head = (c_in // HEAD_SIZE) == (c_out // HEAD_SIZE)
    low = same_head & (local < halves) & (c_in % HEAD_SIZE == local + halves)
    high = same_head & (local >= halves) & (c_in % HEAD_SIZE == local - halves)
    return jnp.where(low, -1.0, jnp.where(high, 1.0, 0.0)).astype(jnp.bfloat16)


def rotate_flat(field, cosine, sine_tab, turn):
    heads = field.shape[1] // HEAD_SIZE
    turned = jnp.dot(field, turn, preferred_element_type=jnp.float32)
    cos_all = jnp.tile(cosine, (1, heads))
    sin_all = jnp.tile(sine_tab, (1, heads))
    return (field.astype(jnp.float32) * cos_all + turned * sin_all).astype(jnp.bfloat16)


def turn_rows(field, cos_rows, sin_rows, turn):
    turned = jnp.dot(field, turn, preferred_element_type=jnp.float32)
    return (field.astype(jnp.float32) * cos_rows + turned * sin_rows).astype(jnp.bfloat16)


def head_select(cols, lanes):
    heads = cols // HEAD_SIZE
    head = jnp.arange(heads, dtype=jnp.int32)[:, None, None]
    col = jnp.arange(cols, dtype=jnp.int32)[None, :, None]
    lane = jnp.arange(lanes, dtype=jnp.int32)[None, None, :]
    return ((col == head * HEAD_SIZE + lane) & (lane < HEAD_SIZE)).astype(jnp.bfloat16)


def attend_kernel(
    q_ref, kn_ref, vn_ref, kc_ref, vc_ref, cos_ref, sin_ref, turn_ref, sel_ref, selt_ref,
    qrank_ref, cache_ok_ref, krank_ref, o_ref, keys_ref, values_ref,
):
    step = pl.program_id(0)
    block = q_ref.shape[0]
    heads = sel_ref.shape[0]

    @pl.when(step == 0)
    def _():
        rotated = turn_rows(kn_ref[...], cos_ref[...], sin_ref[...], turn_ref[...])
        fresh = vn_ref[...]
        for head in range(heads):
            keys_ref[head] = jnp.dot(
                rotated, sel_ref[head], preferred_element_type=jnp.float32
            ).astype(jnp.bfloat16)
            values_ref[head] = jnp.dot(
                fresh, sel_ref[head], preferred_element_type=jnp.float32
            ).astype(jnp.bfloat16)

    here = pl.ds(pl.multiple_of(step * block, block), block)
    query = turn_rows(q_ref[...], cos_ref[here, :], sin_ref[here, :], turn_ref[...])
    score_scale = 1.0 / math.sqrt(HEAD_SIZE)
    cache_ok = cache_ok_ref[...] > 0
    new_ok = krank_ref[...] <= qrank_ref[...]
    contract = (((1,), (1,)), ((), ()))
    total = jnp.zeros(o_ref.shape, jnp.float32)
    for head in range(heads):
        head_query = jnp.dot(query, sel_ref[head], preferred_element_type=jnp.float32).astype(
            jnp.bfloat16
        )
        score_c = lax.dot_general(
            head_query, kc_ref[head], contract, preferred_element_type=jnp.float32
        ) * score_scale
        score_n = lax.dot_general(
            head_query, keys_ref[head], contract, preferred_element_type=jnp.float32
        ) * score_scale
        score_c = jnp.where(cache_ok, score_c, -1e30)
        score_n = jnp.where(new_ok, score_n, -1e30)
        top = jnp.maximum(
            jnp.max(score_c, axis=1, keepdims=True), jnp.max(score_n, axis=1, keepdims=True)
        )
        weight_c = jnp.exp(score_c - top)
        weight_n = jnp.exp(score_n - top)
        whole = jnp.sum(weight_c, axis=1, keepdims=True) + jnp.sum(weight_n, axis=1, keepdims=True)
        prob_c = (weight_c / whole).astype(jnp.bfloat16)
        prob_n = (weight_n / whole).astype(jnp.bfloat16)
        head_out = jnp.dot(prob_c, vc_ref[head], preferred_element_type=jnp.float32) + jnp.dot(
            prob_n, values_ref[head], preferred_element_type=jnp.float32
        )
        total = total + jnp.dot(
            head_out.astype(jnp.bfloat16), selt_ref[head], preferred_element_type=jnp.float32
        )
    o_ref[...] = total.astype(o_ref.dtype)


def attend_slots(query, fresh_keys, fresh_values, cache_keys, cache_values, cos_all, sin_all, turn,
                 q_rank, cache_ok, k_rank, slot_cap):
    rows, cols = query.shape
    block = rows // slot_cap
    span = cache_keys.shape[0]
    heads = cols // HEAD_SIZE
    lanes = 128
    sel = head_select(cols, lanes)
    sel_t = sel.transpose(0, 2, 1)
    split = lambda x: jnp.pad(
        x.reshape(x.shape[0], heads, HEAD_SIZE), ((0, 0), (0, 0), (0, lanes - HEAD_SIZE))
    ).transpose(1, 0, 2)
    whole = lambda i: (0, 0)
    whole3 = lambda i: (0, 0, 0)
    return pl.pallas_call(
        attend_kernel,
        out_shape=jax.ShapeDtypeStruct((block, slot_cap * cols), jnp.bfloat16),
        grid=(slot_cap,),
        in_specs=[
            pl.BlockSpec((block, cols), lambda i: (i, 0)),
            pl.BlockSpec((rows, cols), whole),
            pl.BlockSpec((rows, cols), whole),
            pl.BlockSpec((heads, span, lanes), whole3),
            pl.BlockSpec((heads, span, lanes), whole3),
            pl.BlockSpec((rows, cols), whole),
            pl.BlockSpec((rows, cols), whole),
            pl.BlockSpec((cols, cols), whole),
            pl.BlockSpec((heads, cols, lanes), whole3),
            pl.BlockSpec((heads, lanes, cols), whole3),
            pl.BlockSpec((block, 1), lambda i: (i, 0)),
            pl.BlockSpec((1, span), whole),
            pl.BlockSpec((1, rows), whole),
        ],
        out_specs=pl.BlockSpec((block, cols), lambda i: (0, i)),
        scratch_shapes=[
            pltpu.VMEM((heads, rows, lanes), jnp.bfloat16),
            pltpu.VMEM((heads, rows, lanes), jnp.bfloat16),
        ],
        compiler_params=pltpu.CompilerParams(dimension_semantics=("arbitrary",)),
    )(query, fresh_keys, fresh_values, split(cache_keys), split(cache_values), cos_all, sin_all,
      turn, sel, sel_t, q_rank, cache_ok, k_rank)


def on_device(
    qkv_rows,
    row_request,
    request_owner,
    cached_len,
    page_table,
    kv_pages,
    residual,
    out_weight,
    norm_gain,
):
    row_count = qkv_rows.shape[0]
    parts = qkv_rows.shape[1]
    head_cols = qkv_rows.shape[2]
    heads_here = head_cols // HEAD_SIZE
    devices = lax.axis_size("req")
    slot_cap = SLOT
    buffer_len = devices * slot_cap
    device_ids = jnp.arange(devices, dtype=jnp.int32)
    row_ids = jnp.arange(row_count, dtype=jnp.int32)

    weight_cols = lax.all_to_all(out_weight, "tp", split_axis=1, concat_axis=0, tiled=True)
    owner_dev = request_owner[row_request]
    same_owner = owner_dev[:, None] == owner_dev[None, :]
    slot_in = jnp.sum((same_owner & (row_ids[None, :] < row_ids[:, None])).astype(jnp.int32), axis=1)
    sends_to = owner_dev[:, None] == device_ids[None, :]
    counts = jnp.sum(sends_to.astype(jnp.int32), axis=0)

    pick = (
        sends_to[None, :, :]
        & (slot_in[None, :, None] == jnp.arange(slot_cap, dtype=jnp.int32)[:, None, None])
    ).astype(jnp.bfloat16)
    row_part = jnp.repeat(jnp.arange(parts, dtype=jnp.int32), slot_cap)
    sources = jnp.concatenate(
        [qkv_rows[:, row_part, :], jnp.ones((row_count, 1, head_cols), qkv_rows.dtype)], axis=1
    )
    picks = jnp.concatenate([jnp.tile(pick, (parts, 1, 1)), sends_to[None].astype(jnp.bfloat16)])
    outgoing = jnp.einsum(
        "rid,irc->drc", picks, sources, preferred_element_type=jnp.float32
    ).astype(jnp.bfloat16)
    arrived = lax.all_to_all(outgoing, "req", split_axis=0, concat_axis=0, tiled=True)
    planes = arrived.transpose(1, 0, 2)
    arrived_counts = planes[slot_cap * parts, :, 0].astype(jnp.int32)

    length = cached_len[0]
    pool_pages = kv_pages[page_table[0]]
    cache_span = pool_pages.shape[0] * pool_pages.shape[2]
    cache_keys = pool_pages[:, 0].reshape(cache_span, head_cols)
    cache_values = pool_pages[:, 1].reshape(cache_span, head_cols)
    slot_of = jnp.arange(slot_cap, dtype=jnp.int32)[:, None]
    before = jnp.cumsum(arrived_counts) - arrived_counts
    live_slot = (slot_of < arrived_counts[None, :]).reshape(buffer_len)
    new_rank = (before[None, :] + slot_of).reshape(buffer_len)
    cosine, sine_tab = rope_tables(length + new_rank)
    cos_all = jnp.tile(cosine, (1, heads_here))
    sin_all = jnp.tile(sine_tab, (1, heads_here))
    cache_ok = (jnp.arange(cache_span, dtype=jnp.int32) < length).astype(jnp.int32)[None, :]
    k_rank = jnp.where(live_slot, new_rank, jnp.int32(2**30))[None, :]
    q_rank = new_rank[:, None]
    part_rows = [
        planes[p * slot_cap : (p + 1) * slot_cap].reshape(buffer_len, head_cols)
        for p in range(parts)
    ]
    result = attend_slots(
        part_rows[0], part_rows[1], part_rows[2], cache_keys, cache_values, cos_all, sin_all,
        turn_matrix(head_cols), q_rank, cache_ok, k_rank, slot_cap,
    )
    returned = lax.all_to_all(
        result.reshape(devices, slot_cap * parts, head_cols // parts),
        "req",
        split_axis=0,
        concat_axis=0,
        tiled=True,
    )
    target = owner_dev * slot_cap + slot_in
    attn_rows = returned.reshape(buffer_len, head_cols)[target]
    attn_all = lax.all_gather(attn_rows, "tp", axis=1, tiled=True)
    mixed_cols = jnp.dot(attn_all, weight_cols, preferred_element_type=jnp.float32)
    hidden = residual.astype(jnp.float32) + mixed_cols
    square_part = jnp.sum(hidden * hidden, axis=1)
    tp_size = lax.axis_size("tp")
    square_sum = jnp.sum(
        lax.all_to_all(
            jnp.broadcast_to(square_part[None], (tp_size,) + square_part.shape), "tp", 0, 0, tiled=True
        ),
        axis=0,
    )
    inv_rms = lax.rsqrt(square_sum / D + EPS)
    normed = hidden * inv_rms[:, None] * norm_gain.astype(jnp.float32)[None, :]
    return (hidden.astype(jnp.bfloat16), normed.astype(jnp.bfloat16))


def solution(mesh):
    return jax.shard_map(
        on_device,
        mesh=mesh,
        in_specs=(
            P("req", None, "tp"),
            P("req"),
            P(),
            P("req"),
            P("req", None),
            P("req", None, None, "tp"),
            P("req", "tp"),
            P("tp", None),
            P("tp"),
        ),
        out_specs=(P("req", "tp"), P("req", "tp")),
        check_vma=False,
    )
```
